256 devices in a mesh: gx: 16 (over z, core), gy: 16 (over x, y).
Axes of the slice: x: 4, y: 4, z: 8, core: 2. Of those that a mesh axis runs over, the one named last changes fastest.
Arguments:
- forcing: float32 [4, 8, 4096, 2048], P(None, None, 'gx', 'gy'), may hold values from -150 to 150
- velocity: float32 [2, 4096, 2048], P(None, 'gx', 'gy'), may hold values from -0.6 to 0.6
- viscosity: float32 [4096, 2048], P('gx', 'gy'), may hold values from 0.05 to 0.25
- sound: float32 [4096, 2048], P('gx', 'gy'), may hold values from 0.4 to 1
- coupling: float32 [4, 4, 4096, 2048], P(None, None, 'gx', 'gy'), may hold values from -1.5 to 1.5
Outputs:
- basis: float32 [4, 8, 4096, 2048], P(None, None, 'gx', 'gy')
- factor: float32 [8, 8], replicated
The draws below stay inside these ranges and needn't reach their ends.
All inputs are finite; a program needn't handle non-finite values.
Results may differ from the reference program's by a relative error of at most 0.000055.
Values sent between devices are 32-bit elements; how exact they have to be, the bound alone decides.
No kernel may reach another device: no remote copies, remote signals or barrier semaphores. Data moves between devices by JAX's collectives and lax.ppermute only.
A program may use at most 128 MiB of HBM per device.

```python
import math
import jax
import jax.numpy as jnp
from jax import lax

NVAR = 4
NCOL = 8
NX = 4096
NY = 2048
ROWS = 33554432


def draw_forcing(key, part):
    key_base, key_rough, key_cols = jax.random.split(key, 3)
    xs = jnp.arange(NX, dtype=jnp.float32) / NX
    ys = jnp.arange(NY, dtype=jnp.float32) / NY
    base = jnp.clip(jax.random.normal(key_base, (NVAR, NCOL, NX, NY), jnp.float32), -5.0, 5.0)
    envelope = jnp.exp(0.55 * xs)[:, None] * jnp.exp(0.55 * ys)[None, :]
    rough = jnp.exp(jax.random.uniform(key_rough, (NX, NY), jnp.float32, 0.0, 1.2))
    col_scale = jnp.exp(jax.random.uniform(key_cols, (NCOL,), jnp.float32, 0.0, 1.1))
    return (base * col_scale[None, :, None, None] * (envelope * rough)[None, None]).astype(jnp.float32)


def shard_levels(key, dims, pieces, least, high):
    def one(dim, parts):
        heights = jax.random.uniform(jax.random.fold_in(jax.random.fold_in(key, 6), dim), (parts,), jnp.float32, least / len(pieces), high / len(pieces))
        return jnp.repeat(jnp.exp(heights), dims[dim] // parts).reshape((-1,) + (1,) * (len(dims) - dim - 1))

    factor_of = one(*pieces[0])
    for cut in pieces[1:]:
        factor_of = factor_of * one(*cut)
    return factor_of


def centred(rng, shape, deviation, reach, cuts=(), kind=jnp.bfloat16):
    gain = shard_levels(rng, shape, cuts, -0.22, 0.18) if cuts else 1.0
    values = jax.random.normal(rng, shape, jnp.float32) * deviation * gain
    return jnp.minimum(jnp.maximum(values, -reach), reach).astype(kind)


def setup_inputs(seed: int = 0) -> dict:
    key_of = jax.random.split(jax.random.key(seed), 6)
    forcing = draw_forcing(jax.random.fold_in(key_of[5], 71), 0)
    velocity = jnp.clip(jax.random.uniform(key_of[1], (2, NX, NY), jnp.float32, -0.6, 0.6) * shard_levels(key_of[1], (2, NX, NY), ((1, 16), (2, 16)), -0.4, 0.0), -0.6, 0.6)
    viscosity = jnp.clip(jnp.exp(math.log(0.25) - 1.609438 * jax.random.uniform(key_of[2], (NX, NY), jnp.float32) ** shard_levels(key_of[2], (NX, NY), ((0, 16), (1, 16)), -0.2, 0.2)), 0.05, 0.25)
    sound = jnp.clip(jnp.exp(math.log(1.0) - 0.9162907 * jax.random.uniform(key_of[3], (NX, NY), jnp.float32) ** shard_levels(key_of[3], (NX, NY), ((0, 16), (1, 16)), -0.2, 0.2)), 0.4, 1.0)
    coupling = centred(key_of[4], (NVAR, NVAR, NX, NY), 0.3, 1.5, ((2, 16), (3, 16)), jnp.float32)
    return {"forcing": forcing, "velocity": velocity, "viscosity": viscosity, "sound": sound, "coupling": coupling}


STEP = 0.5

def tendency(padded, velocity, viscosity, sound, coupling):
    center = padded[:, :, 1:-1, 1:-1]
    east = padded[:, :, 2:, 1:-1]
    west = padded[:, :, :-2, 1:-1]
    north = padded[:, :, 1:-1, 2:]
    south = padded[:, :, 1:-1, :-2]
    grad_x = 0.5 * (east - west)
    grad_y = 0.5 * (north - south)
    laplace = east + west + north + south - 4.0 * center
    transport = viscosity * laplace - velocity[0] * grad_x - velocity[1] * grad_y
    divergence = grad_x[1] + grad_y[2]
    acoustic = jnp.stack([-sound * divergence, -sound * grad_x[3], -sound * grad_y[3], -sound * divergence])
    mixing = coupling[:, 0][:, None] * center[0][None]
    for inner in range(1, 4):
        mixing = mixing + coupling[:, inner][:, None] * center[inner][None]
    return transport + acoustic - mixing

def pad_one(field):
    return jnp.pad(field, ((0, 0), (0, 0), (1, 1), (1, 1)))

def advance(state, velocity, viscosity, sound, coupling):
    first = tendency(pad_one(state), velocity, viscosity, sound, coupling) + state
    middle = state + STEP * first
    second = tendency(pad_one(middle), velocity, viscosity, sound, coupling) + state
    return state + 0.5 * STEP * (first + second)

def reference(forcing, velocity, viscosity, sound, coupling):
    columns = jnp.moveaxis(forcing, 1, 0)

    def one_column(column):
        return advance(column[:, None], velocity, viscosity, sound, coupling)[:, 0]
    response = jnp.moveaxis(lax.map(one_column, columns), 0, 1)
    gram = jnp.einsum('vcxy,vdxy->cd', response, response, precision=lax.Precision.HIGHEST) / ROWS
    lower = jnp.linalg.cholesky(gram)
    identity = jnp.eye(NCOL, dtype=lower.dtype)
    inverse = lax.linalg.triangular_solve(lower, identity, left_side=True, lower=True)
    basis = jnp.einsum('cd,vdxy->vcxy', inverse, response, precision=lax.Precision.HIGHEST)
    return (basis, lower.T)
```

```python
import jax
import jax.numpy as jnp
from jax import lax
from jax.sharding import PartitionSpec as P

STEP = 0.5


def with_halo(cells, sides, width):
    for axis, dim in sides:
        count = lax.axis_size(axis)
        ends = count - 1
        head = lax.slice_in_dim(cells, 0, width, axis=dim)
        tail = lax.slice_in_dim(cells, cells.shape[dim] - width, cells.shape[dim], axis=dim)
        cells = jnp.concatenate(
            [
                lax.ppermute(tail, axis, [(i, (i + 1) % count) for i in range(ends)]),
                cells,
                lax.ppermute(head, axis, [((i + 1) % count, i) for i in range(ends)]),
            ],
            axis=dim,
        )
    return cells


def tendency(padded, velocity, viscosity, sound, coupling):
    center = padded[:, :, 1:-1, 1:-1]
    east = padded[:, :, 2:, 1:-1]
    west = padded[:, :, :-2, 1:-1]
    north = padded[:, :, 1:-1, 2:]
    south = padded[:, :, 1:-1, :-2]
    grad_x = 0.5 * (east - west)
    grad_y = 0.5 * (north - south)
    laplace = east + west + north + south - 4.0 * center
    transport = viscosity * laplace - velocity[0] * grad_x - velocity[1] * grad_y
    divergence = grad_x[1] + grad_y[2]
    acoustic = jnp.stack(
        [-sound * divergence, -sound * grad_x[3], -sound * grad_y[3], -sound * divergence]
    )
    mixing = coupling[:, 0][:, None] * center[0][None]
    for inner in range(1, 4):
        mixing = mixing + coupling[:, inner][:, None] * center[inner][None]
    return transport + acoustic - mixing


def all_sum(value):
    for axis in ("gy", "gx"):
        count = lax.axis_size(axis)
        bit = 1
        while bit < count:
            value = value + lax.ppermute(value, axis, [(i, i ^ bit) for i in range(count)])
            bit *= 2
    return value


def extend(state):
    return with_halo(state, (("gx", 2), ("gy", 3)), 1)


def local(forcing, velocity, viscosity, sound, coupling):
    first = tendency(extend(forcing), velocity, viscosity, sound, coupling) + forcing
    middle = forcing + STEP * first
    second = tendency(extend(middle), velocity, viscosity, sound, coupling) + forcing
    response = forcing + 0.5 * STEP * (first + second)
    rows_total = float(
        4 * forcing.shape[2] * forcing.shape[3] * lax.axis_size("gx") * lax.axis_size("gy")
    )
    local_gram = (
        jnp.einsum("vcxy,vdxy->cd", response, response, precision=lax.Precision.HIGHEST)
        / rows_total
    )
    lower = jnp.linalg.cholesky(all_sum(local_gram))
    identity = jnp.eye(lower.shape[0], dtype=lower.dtype)
    inverse = lax.linalg.triangular_solve(lower, identity, left_side=True, lower=True)
    basis = jnp.einsum("cd,vdxy->vcxy", inverse, response, precision=lax.Precision.HIGHEST)
    return (basis, lower.T)


def solution(mesh):
    in_specs = (
        P(None, None, "gx", "gy"),
        P(None, "gx", "gy"),
        P("gx", "gy"),
        P("gx", "gy"),
        P(None, None, "gx", "gy"),
    )
    out_specs = (P(None, None, "gx", "gy"), P())
    return jax.shard_map(local, mesh=mesh, in_specs=in_specs, out_specs=out_specs, check_vma=False)
```

```python
import jax
import jax.numpy as jnp
from jax import lax
from jax.experimental import pallas as pl
from jax.experimental.pallas import tpu as pltpu
from jax.sharding import PartitionSpec as P

STEP = 0.5
NV = 4


def all_sum(value):
    for axis in ("gy", "gx"):
        count = lax.axis_size(axis)
        bit = 1
        while bit < count:
            value = value + lax.ppermute(value, axis, [(i, i ^ bit) for i in range(count)])
            bit *= 2
    return value


def exchange(low, high, axis):
    count = lax.axis_size(axis)
    from_below = lax.ppermute(high, axis, [(i, i + 1) for i in range(count - 1)])
    from_above = lax.ppermute(low, axis, [(i + 1, i) for i in range(count - 1)])
    return from_below, from_above


def operator(q, west, east, south, north, vel_ref, visc_ref, snd_ref, coup_ref):
    nx, ny = q[0].shape
    rows = lax.broadcasted_iota(jnp.int32, (nx, ny), 0)
    lanes = lax.broadcasted_iota(jnp.int32, (nx, ny), 1)
    half = lax.broadcasted_iota(jnp.int32, (ny, nx), 0) < ny // 2
    vel0 = vel_ref[0]
    vel1 = vel_ref[1]
    visc = visc_ref[...]
    snd = snd_ref[...]
    grad_x, grad_y, transport = [], [], []
    for v in range(NV):
        field = q[v]
        columns = jnp.where(half, south[v], north[v]).T
        e = jnp.where(rows == nx - 1, east[v], pltpu.roll(field, nx - 1, 0))
        w = jnp.where(rows == 0, west[v], pltpu.roll(field, 1, 0))
        n = jnp.where(lanes == ny - 1, columns, pltpu.roll(field, ny - 1, 1))
        s = jnp.where(lanes == 0, columns, pltpu.roll(field, 1, 1))
        gx = 0.5 * (e - w)
        gy = 0.5 * (n - s)
        laplace = e + w + n + s - 4.0 * field
        grad_x.append(gx)
        grad_y.append(gy)
        transport.append(visc * laplace - vel0 * gx - vel1 * gy)
    divergence = grad_x[1] + grad_y[2]
    acoustic = [-snd * divergence, -snd * grad_x[3], -snd * grad_y[3], -snd * divergence]
    out = []
    for w_ in range(NV):
        mixing = coup_ref[w_, 0] * q[0]
        for inner in range(1, NV):
            mixing = mixing + coup_ref[w_, inner] * q[inner]
        out.append(transport[w_] + acoustic[w_] - mixing)
    return out


def stage_one(f_ref, vel_ref, visc_ref, snd_ref, coup_ref, hw_ref, he_ref, hs_ref, hn_ref,
              first_ref, mid_ref, mw_ref, me_ref, ms_ref, mn_ref):
    q = [f_ref[v, 0] for v in range(NV)]
    west = [hw_ref[0, v:v + 1, :] for v in range(NV)]
    east = [he_ref[0, v:v + 1, :] for v in range(NV)]
    south = [hs_ref[0, v:v + 1, :] for v in range(NV)]
    north = [hn_ref[0, v:v + 1, :] for v in range(NV)]
    lq = operator(q, west, east, south, north, vel_ref, visc_ref, snd_ref, coup_ref)
    nx, ny = q[0].shape
    for v in range(NV):
        first = lq[v] + q[v]
        middle = q[v] + STEP * first
        first_ref[v, 0] = first
        mid_ref[v, 0] = middle
        mw_ref[0, v:v + 1, :] = middle[0:1, :]
        me_ref[0, v:v + 1, :] = middle[nx - 1:nx, :]
        flipped = middle.T
        ms_ref[0, v:v + 1, :] = flipped[0:1, :]
        mn_ref[0, v:v + 1, :] = flipped[ny - 1:ny, :]


def stage_two(f_ref, first_ref, mid_ref, vel_ref, visc_ref, snd_ref, coup_ref, hw_ref, he_ref, hs_ref, hn_ref,
              resp_ref, gram_ref):
    c = pl.program_id(0)
    ncol = resp_ref.shape[1]
    nx, ny = f_ref.shape[2], f_ref.shape[3]
    q = [mid_ref[v, 0] for v in range(NV)]
    west = [hw_ref[0, v:v + 1, :] for v in range(NV)]
    east = [he_ref[0, v:v + 1, :] for v in range(NV)]
    south = [hs_ref[0, v:v + 1, :] for v in range(NV)]
    north = [hn_ref[0, v:v + 1, :] for v in range(NV)]
    lq = operator(q, west, east, south, north, vel_ref, visc_ref, snd_ref, coup_ref)
    resp = []
    for v in range(NV):
        forcing = f_ref[v, 0]
        second = lq[v] + forcing
        r = forcing + 0.5 * STEP * (first_ref[v, 0] + second)
        resp_ref[v, pl.ds(c, 1)] = r[None]
        resp.append(r)
    for d in range(ncol):
        @pl.when(d <= c)
        def _():
            acc = None
            for v in range(NV):
                prod = (resp_ref[v, d] * resp[v]).reshape(nx // 8, 8, ny).sum(axis=0)
                acc = prod if acc is None else acc + prod
            gram_ref[c * ncol + d] = acc
            gram_ref[d * ncol + c] = acc


def combine(inv_ref, r_ref, out_ref):
    ncol = r_ref.shape[1]
    rs = [r_ref[0, d] for d in range(ncol)]
    for c in range(ncol):
        acc = inv_ref[c, 0] * rs[0]
        for d in range(1, ncol):
            acc = acc + inv_ref[c, d] * rs[d]
        out_ref[0, c] = acc


def local(forcing, velocity, viscosity, sound, coupling):
    nv, ncol, nx, ny = forcing.shape
    f32 = jnp.float32
    whole = lambda shape: pl.BlockSpec(shape, lambda c: (0,) * len(shape))
    column = pl.BlockSpec((nv, 1, nx, ny), lambda c: (0, c, 0, 0))
    edge_x = pl.BlockSpec((1, nv, ny), lambda c: (c, 0, 0))
    edge_y = pl.BlockSpec((1, nv, nx), lambda c: (c, 0, 0))
    coef_specs = [whole((2, nx, ny)), whole((nx, ny)), whole((nx, ny)), whole((nv, nv, nx, ny))]
    params = pltpu.CompilerParams(vmem_limit_bytes=60 * 1024 * 1024)

    def by_column(a):
        return jnp.transpose(a, (1, 0, 2))

    hw, he = exchange(by_column(forcing[:, :, 0, :]), by_column(forcing[:, :, nx - 1, :]), "gx")
    hs, hn = exchange(by_column(forcing[:, :, :, 0]), by_column(forcing[:, :, :, ny - 1]), "gy")

    first, middle, mw, me, ms, mn = pl.pallas_call(
        stage_one,
        grid=(ncol,),
        in_specs=[column] + coef_specs + [edge_x, edge_x, edge_y, edge_y],
        out_specs=[column, column, edge_x, edge_x, edge_y, edge_y],
        out_shape=[
            jax.ShapeDtypeStruct(forcing.shape, f32),
            jax.ShapeDtypeStruct(forcing.shape, f32),
            jax.ShapeDtypeStruct((ncol, nv, ny), f32),
            jax.ShapeDtypeStruct((ncol, nv, ny), f32),
            jax.ShapeDtypeStruct((ncol, nv, nx), f32),
            jax.ShapeDtypeStruct((ncol, nv, nx), f32),
        ],
        compiler_params=params,
    )(forcing, velocity, viscosity, sound, coupling, hw, he, hs, hn)

    hw2, he2 = exchange(mw, me, "gx")
    hs2, hn2 = exchange(ms, mn, "gy")

    response, partial = pl.pallas_call(
        stage_two,
        grid=(ncol,),
        in_specs=[column, column, column] + coef_specs + [edge_x, edge_x, edge_y, edge_y],
        out_specs=[whole(forcing.shape), whole((ncol * ncol, 8, ny))],
        out_shape=[
            jax.ShapeDtypeStruct(forcing.shape, f32),
            jax.ShapeDtypeStruct((ncol * ncol, 8, ny), f32),
        ],
        compiler_params=pltpu.CompilerParams(
            vmem_limit_bytes=60 * 1024 * 1024, dimension_semantics=("arbitrary",)
        ),
    )(forcing, first, middle, velocity, viscosity, sound, coupling, hw2, he2, hs2, hn2)

    rows_total = float(nv * nx * ny * lax.axis_size("gx") * lax.axis_size("gy"))
    local_gram = jnp.sum(partial, axis=(1, 2)).reshape(ncol, ncol) / rows_total
    lower = jnp.linalg.cholesky(all_sum(local_gram))
    identity = jnp.eye(lower.shape[0], dtype=lower.dtype)
    inverse = lax.linalg.triangular_solve(lower, identity, left_side=True, lower=True)

    basis = pl.pallas_call(
        combine,
        grid=(nv,),
        in_specs=[
            pl.BlockSpec(memory_space=pltpu.SMEM),
            pl.BlockSpec((1, ncol, nx, ny), lambda v: (v, 0, 0, 0)),
        ],
        out_specs=pl.BlockSpec((1, ncol, nx, ny), lambda v: (v, 0, 0, 0)),
        out_shape=jax.ShapeDtypeStruct(forcing.shape, f32),
        compiler_params=params,
    )(inverse, response)
    return (basis, lower.T)


def solution(mesh):
    in_specs = (
        P(None, None, "gx", "gy"),
        P(None, "gx", "gy"),
        P("gx", "gy"),
        P("gx", "gy"),
        P(None, None, "gx", "gy"),
    )
    out_specs = (P(None, None, "gx", "gy"), P())
    return jax.shard_map(local, mesh=mesh, in_specs=in_specs, out_specs=out_specs, check_vma=False)
```

```python
import jax
import jax.numpy as jnp
from jax import lax
from jax.experimental import pallas as pl
from jax.experimental.pallas import tpu as pltpu
from jax.sharding import PartitionSpec as P

STEP = 0.5
NV = 4


def all_sum(value):
    for axis in ("gy", "gx"):
        count = lax.axis_size(axis)
        bit = 1
        while bit < count:
            value = value + lax.ppermute(value, axis, [(i, i ^ bit) for i in range(count)])
            bit *= 2
    return value


def exchange(low, high, axis):
    count = lax.axis_size(axis)
    from_below = lax.ppermute(high, axis, [(i, i + 1) for i in range(count - 1)])
    from_above = lax.ppermute(low, axis, [(i + 1, i) for i in range(count - 1)])
    return from_below, from_above


def operator(q, west, east, south, north, vel_ref, visc_ref, snd_ref, coup_ref):
    nx, ny = q[0].shape
    rows = lax.broadcasted_iota(jnp.int32, (nx, ny), 0)
    lanes = lax.broadcasted_iota(jnp.int32, (nx, ny), 1)
    half = lax.broadcasted_iota(jnp.int32, (ny, nx), 0) < ny // 2
    vel0 = vel_ref[0]
    vel1 = vel_ref[1]
    visc = visc_ref[...]
    snd = snd_ref[...]
    grad_x, grad_y, transport = [], [], []
    for v in range(NV):
        field = q[v]
        columns = jnp.where(half, south[v], north[v]).T
        e = jnp.where(rows == nx - 1, east[v], pltpu.roll(field, nx - 1, 0))
        w = jnp.where(rows == 0, west[v], pltpu.roll(field, 1, 0))
        n = jnp.where(lanes == ny - 1, columns, pltpu.roll(field, ny - 1, 1))
        s = jnp.where(lanes == 0, columns, pltpu.roll(field, 1, 1))
        gx = 0.5 * (e - w)
        gy = 0.5 * (n - s)
        laplace = e + w + n + s - 4.0 * field
        grad_x.append(gx)
        grad_y.append(gy)
        transport.append(visc * laplace - vel0 * gx - vel1 * gy)
    divergence = grad_x[1] + grad_y[2]
    acoustic = [-snd * divergence, -snd * grad_x[3], -snd * grad_y[3], -snd * divergence]
    out = []
    for w_ in range(NV):
        mixing = coup_ref[w_, 0] * q[0]
        for inner in range(1, NV):
            mixing = mixing + coup_ref[w_, inner] * q[inner]
        out.append(transport[w_] + acoustic[w_] - mixing)
    return out


def stage_one(f_ref, vel_ref, visc_ref, snd_ref, coup_ref, hw_ref, he_ref, hs_ref, hn_ref,
              first_ref, mid_ref, mw_ref, me_ref, ms_ref, mn_ref):
    q = [f_ref[v, 0] for v in range(NV)]
    west = [hw_ref[0, v:v + 1, :] for v in range(NV)]
    east = [he_ref[0, v:v + 1, :] for v in range(NV)]
    south = [hs_ref[0, v:v + 1, :] for v in range(NV)]
    north = [hn_ref[0, v:v + 1, :] for v in range(NV)]
    lq = operator(q, west, east, south, north, vel_ref, visc_ref, snd_ref, coup_ref)
    nx, ny = q[0].shape
    for v in range(NV):
        first = lq[v] + q[v]
        middle = q[v] + STEP * first
        first_ref[v, 0] = first
        mid_ref[v, 0] = middle
        mw_ref[0, v:v + 1, :] = middle[0:1, :]
        me_ref[0, v:v + 1, :] = middle[nx - 1:nx, :]
        flipped = middle.T
        ms_ref[0, v:v + 1, :] = flipped[0:1, :]
        mn_ref[0, v:v + 1, :] = flipped[ny - 1:ny, :]


def stage_two(f_ref, first_ref, mid_ref, vel_ref, visc_ref, snd_ref, coup_ref, hw_ref, he_ref, hs_ref, hn_ref,
              resp_ref, gram_ref):
    c = pl.program_id(0)
    ncol = resp_ref.shape[1]
    nx, ny = f_ref.shape[2], f_ref.shape[3]
    q = [mid_ref[v, 0] for v in range(NV)]
    west = [hw_ref[0, v:v + 1, :] for v in range(NV)]
    east = [he_ref[0, v:v + 1, :] for v in range(NV)]
    south = [hs_ref[0, v:v + 1, :] for v in range(NV)]
    north = [hn_ref[0, v:v + 1, :] for v in range(NV)]
    lq = operator(q, west, east, south, north, vel_ref, visc_ref, snd_ref, coup_ref)
    resp = []
    for v in range(NV):
        forcing = f_ref[v, 0]
        second = lq[v] + forcing
        r = forcing + 0.5 * STEP * (first_ref[v, 0] + second)
        resp_ref[v, pl.ds(c, 1)] = r[None]
        resp.append(r)
    for d in range(ncol):
        @pl.when(d <= c)
        def _():
            acc = None
            for v in range(NV):
                prod = (resp_ref[v, d] * resp[v]).reshape(nx // 8, 8, ny).sum(axis=0)
                acc = prod if acc is None else acc + prod
            total = jnp.sum(acc)
            gram_ref[c * ncol + d] = total
            gram_ref[d * ncol + c] = total


def edges(f_ref, w_ref, e_ref, s_ref, n_ref):
    nx, ny = f_ref.shape[2], f_ref.shape[3]
    for v in range(NV):
        field = f_ref[v, 0]
        w_ref[0, v:v + 1, :] = field[0:1, :]
        e_ref[0, v:v + 1, :] = field[nx - 1:nx, :]
        flipped = field.T
        s_ref[0, v:v + 1, :] = flipped[0:1, :]
        n_ref[0, v:v + 1, :] = flipped[ny - 1:ny, :]


def combine(inv_ref, r_ref, out_ref):
    ncol = r_ref.shape[1]
    rs = [r_ref[0, d] for d in range(ncol)]
    for c in range(ncol):
        acc = inv_ref[c, 0] * rs[0]
        for d in range(1, ncol):
            acc = acc + inv_ref[c, d] * rs[d]
        out_ref[0, c] = acc


def local(forcing, velocity, viscosity, sound, coupling):
    nv, ncol, nx, ny = forcing.shape
    f32 = jnp.float32
    whole = lambda shape: pl.BlockSpec(shape, lambda c: (0,) * len(shape))
    column = pl.BlockSpec((nv, 1, nx, ny), lambda c: (0, c, 0, 0))
    edge_x = pl.BlockSpec((1, nv, ny), lambda c: (c, 0, 0))
    edge_y = pl.BlockSpec((1, nv, nx), lambda c: (c, 0, 0))
    coef_specs = [whole((2, nx, ny)), whole((nx, ny)), whole((nx, ny)), whole((nv, nv, nx, ny))]
    params = pltpu.CompilerParams(vmem_limit_bytes=60 * 1024 * 1024)

    fw, fe, fs, fn = pl.pallas_call(
        edges,
        grid=(ncol,),
        in_specs=[column],
        out_specs=[edge_x, edge_x, edge_y, edge_y],
        out_shape=[
            jax.ShapeDtypeStruct((ncol, nv, ny), f32),
            jax.ShapeDtypeStruct((ncol, nv, ny), f32),
            jax.ShapeDtypeStruct((ncol, nv, nx), f32),
            jax.ShapeDtypeStruct((ncol, nv, nx), f32),
        ],
        compiler_params=params,
    )(forcing)
    hw, he = exchange(fw, fe, "gx")
    hs, hn = exchange(fs, fn, "gy")

    first, middle, mw, me, ms, mn = pl.pallas_call(
        stage_one,
        grid=(ncol,),
        in_specs=[column] + coef_specs + [edge_x, edge_x, edge_y, edge_y],
        out_specs=[column, column, edge_x, edge_x, edge_y, edge_y],
        out_shape=[
            jax.ShapeDtypeStruct(forcing.shape, f32),
            jax.ShapeDtypeStruct(forcing.shape, f32),
            jax.ShapeDtypeStruct((ncol, nv, ny), f32),
            jax.ShapeDtypeStruct((ncol, nv, ny), f32),
            jax.ShapeDtypeStruct((ncol, nv, nx), f32),
            jax.ShapeDtypeStruct((ncol, nv, nx), f32),
        ],
        compiler_params=params,
    )(forcing, velocity, viscosity, sound, coupling, hw, he, hs, hn)

    hw2, he2 = exchange(mw, me, "gx")
    hs2, hn2 = exchange(ms, mn, "gy")

    response, partial = pl.pallas_call(
        stage_two,
        grid=(ncol,),
        in_specs=[column, column, column] + coef_specs + [edge_x, edge_x, edge_y, edge_y],
        out_specs=[whole(forcing.shape), pl.BlockSpec(memory_space=pltpu.SMEM)],
        out_shape=[
            jax.ShapeDtypeStruct(forcing.shape, f32),
            jax.ShapeDtypeStruct((ncol * ncol,), f32),
        ],
        compiler_params=pltpu.CompilerParams(
            vmem_limit_bytes=60 * 1024 * 1024, dimension_semantics=("arbitrary",)
        ),
    )(forcing, first, middle, velocity, viscosity, sound, coupling, hw2, he2, hs2, hn2)

    rows_total = float(nv * nx * ny * lax.axis_size("gx") * lax.axis_size("gy"))
    local_gram = partial.reshape(ncol, ncol) / rows_total
    lower = jnp.linalg.cholesky(all_sum(local_gram))
    identity = jnp.eye(lower.shape[0], dtype=lower.dtype)
    inverse = lax.linalg.triangular_solve(lower, identity, left_side=True, lower=True)

    basis = pl.pallas_call(
        combine,
        grid=(nv,),
        in_specs=[
            pl.BlockSpec(memory_space=pltpu.SMEM),
            pl.BlockSpec((1, ncol, nx, ny), lambda v: (v, 0, 0, 0)),
        ],
        out_specs=pl.BlockSpec((1, ncol, nx, ny), lambda v: (v, 0, 0, 0)),
        out_shape=jax.ShapeDtypeStruct(forcing.shape, f32),
        compiler_params=params,
    )(inverse, response)
    return (basis, lower.T)


def solution(mesh):
    in_specs = (
        P(None, None, "gx", "gy"),
        P(None, "gx", "gy"),
        P("gx", "gy"),
        P("gx", "gy"),
        P(None, None, "gx", "gy"),
    )
    out_specs = (P(None, None, "gx", "gy"), P())
    return jax.shard_map(local, mesh=mesh, in_specs=in_specs, out_specs=out_specs, check_vma=False)
```

```python
import jax
import jax.numpy as jnp
from jax import lax
from jax.experimental import pallas as pl
from jax.experimental.pallas import tpu as pltpu
from jax.sharding import PartitionSpec as P

STEP = 0.5
NV = 4


def all_sum(value):
    for axis in ("gy", "gx"):
        count = lax.axis_size(axis)
        bit = 1
        while bit < count:
            value = value + lax.ppermute(value, axis, [(i, i ^ bit) for i in range(count)])
            bit *= 2
    return value


def exchange(low, high, axis):
    count = lax.axis_size(axis)
    from_below = lax.ppermute(high, axis, [(i, i + 1) for i in range(count - 1)])
    from_above = lax.ppermute(low, axis, [(i + 1, i) for i in range(count - 1)])
    return from_below, from_above


def selector(ny):
    r = lax.broadcasted_iota(jnp.int32, (8, ny), 0)
    y = lax.broadcasted_iota(jnp.int32, (8, ny), 1)
    return jnp.where(((r == 0) & (y == 0)) | ((r == 1) & (y == ny - 1)), 1.0, 0.0).astype(jnp.float32)


def pick_columns(field, sel):
    return lax.dot_general(sel, field, (((1,), (1,)), ((), ())), precision=lax.Precision.HIGHEST,
                           preferred_element_type=jnp.float32)


def place_columns(low, high, sel):
    nx = low.shape[1]
    r = lax.broadcasted_iota(jnp.int32, (8, nx), 0)
    h = jnp.where(r == 0, low, jnp.where(r == 1, high, 0.0))
    return lax.dot_general(h, sel, (((0,), (0,)), ((), ())), precision=lax.Precision.HIGHEST,
                           preferred_element_type=jnp.float32)


def operator(q, west, east, south, north, vel_ref, visc_ref, snd_ref, coup_ref):
    nx, ny = q[0].shape
    rows = lax.broadcasted_iota(jnp.int32, (nx, ny), 0)
    lanes = lax.broadcasted_iota(jnp.int32, (nx, ny), 1)
    sel = selector(ny)
    vel0 = vel_ref[0]
    vel1 = vel_ref[1]
    visc = visc_ref[...]
    snd = snd_ref[...]
    grad_x, grad_y, transport = [], [], []
    for v in range(NV):
        field = q[v]
        columns = place_columns(south[v], north[v], sel)
        e = jnp.where(rows == nx - 1, east[v], pltpu.roll(field, nx - 1, 0))
        w = jnp.where(rows == 0, west[v], pltpu.roll(field, 1, 0))
        n = jnp.where(lanes == ny - 1, columns, pltpu.roll(field, ny - 1, 1))
        s = jnp.where(lanes == 0, columns, pltpu.roll(field, 1, 1))
        gx = 0.5 * (e - w)
        gy = 0.5 * (n - s)
        laplace = e + w + n + s - 4.0 * field
        grad_x.append(gx)
        grad_y.append(gy)
        transport.append(visc * laplace - vel0 * gx - vel1 * gy)
    divergence = grad_x[1] + grad_y[2]
    acoustic = [-snd * divergence, -snd * grad_x[3], -snd * grad_y[3], -snd * divergence]
    out = []
    for w_ in range(NV):
        mixing = coup_ref[w_, 0] * q[0]
        for inner in range(1, NV):
            mixing = mixing + coup_ref[w_, inner] * q[inner]
        out.append(transport[w_] + acoustic[w_] - mixing)
    return out


def stage_one(f_ref, vel_ref, visc_ref, snd_ref, coup_ref, hw_ref, he_ref, hs_ref, hn_ref,
              first_ref, mid_ref, mw_ref, me_ref, ms_ref, mn_ref):
    q = [f_ref[v, 0] for v in range(NV)]
    west = [hw_ref[0, v:v + 1, :] for v in range(NV)]
    east = [he_ref[0, v:v + 1, :] for v in range(NV)]
    south = [hs_ref[0, v:v + 1, :] for v in range(NV)]
    north = [hn_ref[0, v:v + 1, :] for v in range(NV)]
    lq = operator(q, west, east, south, north, vel_ref, visc_ref, snd_ref, coup_ref)
    nx, ny = q[0].shape
    for v in range(NV):
        first = lq[v] + q[v]
        middle = q[v] + STEP * first
        first_ref[v, 0] = first
        mid_ref[v, 0] = middle
        mw_ref[0, v:v + 1, :] = middle[0:1, :]
        me_ref[0, v:v + 1, :] = middle[nx - 1:nx, :]
        picked = pick_columns(middle, selector(ny))
        ms_ref[0, v:v + 1, :] = picked[0:1, :]
        mn_ref[0, v:v + 1, :] = picked[1:2, :]


def stage_two(f_ref, first_ref, mid_ref, vel_ref, visc_ref, snd_ref, coup_ref, hw_ref, he_ref, hs_ref, hn_ref,
              resp_ref, gram_ref):
    c = pl.program_id(0)
    ncol = resp_ref.shape[1]
    nx, ny = f_ref.shape[2], f_ref.shape[3]
    q = [mid_ref[v, 0] for v in range(NV)]
    west = [hw_ref[0, v:v + 1, :] for v in range(NV)]
    east = [he_ref[0, v:v + 1, :] for v in range(NV)]
    south = [hs_ref[0, v:v + 1, :] for v in range(NV)]
    north = [hn_ref[0, v:v + 1, :] for v in range(NV)]
    lq = operator(q, west, east, south, north, vel_ref, visc_ref, snd_ref, coup_ref)
    resp = []
    for v in range(NV):
        forcing = f_ref[v, 0]
        second = lq[v] + forcing
        r = forcing + 0.5 * STEP * (first_ref[v, 0] + second)
        resp_ref[v, pl.ds(c, 1)] = r[None]
        resp.append(r)
    for d in range(ncol):
        @pl.when(d <= c)
        def _():
            acc = None
            for v in range(NV):
                prod = (resp_ref[v, d] * resp[v]).reshape(nx // 8, 8, ny).sum(axis=0)
                acc = prod if acc is None else acc + prod
            row = jnp.sum(acc, axis=0, keepdims=True)
            gram_ref[pl.ds(c * ncol + d, 1), :] = row
            gram_ref[pl.ds(d * ncol + c, 1), :] = row


def edges(f_ref, w_ref, e_ref, s_ref, n_ref):
    nx, ny = f_ref.shape[2], f_ref.shape[3]
    for v in range(NV):
        field = f_ref[v, 0]
        w_ref[0, v:v + 1, :] = field[0:1, :]
        e_ref[0, v:v + 1, :] = field[nx - 1:nx, :]
        picked = pick_columns(field, selector(ny))
        s_ref[0, v:v + 1, :] = picked[0:1, :]
        n_ref[0, v:v + 1, :] = picked[1:2, :]


def combine(inv_ref, r_ref, out_ref):
    ncol = r_ref.shape[1]
    rs = [r_ref[0, d] for d in range(ncol)]
    for c in range(ncol):
        acc = inv_ref[c, 0] * rs[0]
        for d in range(1, ncol):
            acc = acc + inv_ref[c, d] * rs[d]
        out_ref[0, c] = acc


def local(forcing, velocity, viscosity, sound, coupling):
    nv, ncol, nx, ny = forcing.shape
    f32 = jnp.float32
    whole = lambda shape: pl.BlockSpec(shape, lambda c: (0,) * len(shape))
    column = pl.BlockSpec((nv, 1, nx, ny), lambda c: (0, c, 0, 0))
    edge_x = pl.BlockSpec((1, nv, ny), lambda c: (c, 0, 0))
    edge_y = pl.BlockSpec((1, nv, nx), lambda c: (c, 0, 0))
    coef_specs = [whole((2, nx, ny)), whole((nx, ny)), whole((nx, ny)), whole((nv, nv, nx, ny))]
    params = pltpu.CompilerParams(vmem_limit_bytes=60 * 1024 * 1024)

    fw, fe, fs, fn = pl.pallas_call(
        edges,
        grid=(ncol,),
        in_specs=[column],
        out_specs=[edge_x, edge_x, edge_y, edge_y],
        out_shape=[
            jax.ShapeDtypeStruct((ncol, nv, ny), f32),
            jax.ShapeDtypeStruct((ncol, nv, ny), f32),
            jax.ShapeDtypeStruct((ncol, nv, nx), f32),
            jax.ShapeDtypeStruct((ncol, nv, nx), f32),
        ],
        compiler_params=params,
    )(forcing)
    hw, he = exchange(fw, fe, "gx")
    hs, hn = exchange(fs, fn, "gy")

    first, middle, mw, me, ms, mn = pl.pallas_call(
        stage_one,
        grid=(ncol,),
        in_specs=[column] + coef_specs + [edge_x, edge_x, edge_y, edge_y],
        out_specs=[column, column, edge_x, edge_x, edge_y, edge_y],
        out_shape=[
            jax.ShapeDtypeStruct(forcing.shape, f32),
            jax.ShapeDtypeStruct(forcing.shape, f32),
            jax.ShapeDtypeStruct((ncol, nv, ny), f32),
            jax.ShapeDtypeStruct((ncol, nv, ny), f32),
            jax.ShapeDtypeStruct((ncol, nv, nx), f32),
            jax.ShapeDtypeStruct((ncol, nv, nx), f32),
        ],
        compiler_params=params,
    )(forcing, velocity, viscosity, sound, coupling, hw, he, hs, hn)

    hw2, he2 = exchange(mw, me, "gx")
    hs2, hn2 = exchange(ms, mn, "gy")

    response, partial = pl.pallas_call(
        stage_two,
        grid=(ncol,),
        in_specs=[column, column, column] + coef_specs + [edge_x, edge_x, edge_y, edge_y],
        out_specs=[whole(forcing.shape), whole((ncol * ncol, ny))],
        out_shape=[
            jax.ShapeDtypeStruct(forcing.shape, f32),
            jax.ShapeDtypeStruct((ncol * ncol, ny), f32),
        ],
        compiler_params=pltpu.CompilerParams(
            vmem_limit_bytes=60 * 1024 * 1024, dimension_semantics=("arbitrary",)
        ),
    )(forcing, first, middle, velocity, viscosity, sound, coupling, hw2, he2, hs2, hn2)

    rows_total = float(nv * nx * ny * lax.axis_size("gx") * lax.axis_size("gy"))
    local_gram = jnp.sum(partial, axis=1).reshape(ncol, ncol) / rows_total
    lower = jnp.linalg.cholesky(all_sum(local_gram))
    identity = jnp.eye(lower.shape[0], dtype=lower.dtype)
    inverse = lax.linalg.triangular_solve(lower, identity, left_side=True, lower=True)

    basis = pl.pallas_call(
        combine,
        grid=(nv,),
        in_specs=[
            pl.BlockSpec(memory_space=pltpu.SMEM),
            pl.BlockSpec((1, ncol, nx, ny), lambda v: (v, 0, 0, 0)),
        ],
        out_specs=pl.BlockSpec((1, ncol, nx, ny), lambda v: (v, 0, 0, 0)),
        out_shape=jax.ShapeDtypeStruct(forcing.shape, f32),
        compiler_params=params,
    )(inverse, response)
    return (basis, lower.T)


def solution(mesh):
    in_specs = (
        P(None, None, "gx", "gy"),
        P(None, "gx", "gy"),
        P("gx", "gy"),
        P("gx", "gy"),
        P(None, None, "gx", "gy"),
    )
    out_specs = (P(None, None, "gx", "gy"), P())
    return jax.shard_map(local, mesh=mesh, in_specs=in_specs, out_specs=out_specs, check_vma=False)
```

```python
import jax
import jax.numpy as jnp
from jax import lax
from jax.experimental import pallas as pl
from jax.experimental.pallas import tpu as pltpu
from jax.sharding import PartitionSpec as P

STEP = 0.5
NV = 4


def all_sum(value):
    for axis in ("gy", "gx"):
        count = lax.axis_size(axis)
        bit = 1
        while bit < count:
            value = value + lax.ppermute(value, axis, [(i, i ^ bit) for i in range(count)])
            bit *= 2
    return value


def exchange(low, high, axis):
    count = lax.axis_size(axis)
    from_below = lax.ppermute(high, axis, [(i, i + 1) for i in range(count - 1)])
    from_above = lax.ppermute(low, axis, [(i + 1, i) for i in range(count - 1)])
    return from_below, from_above


def pack(pack_ref, fields, c):
    nx, ny = fields[0].shape
    lanes = lax.broadcasted_iota(jnp.int32, (nx, ny), 1)
    cur = pack_ref[...]
    for v, field in enumerate(fields):
        lo = 2 * NV * c + 2 * v
        cur = jnp.where(lanes == lo, pltpu.roll(field, lo, 1), cur)
        cur = jnp.where(lanes == lo + 1, pltpu.roll(field, lo + 2, 1), cur)
    pack_ref[...] = cur


def send_packed(pack_ref, g_ref):
    g_ref[...] = pack_ref[...].T[0:g_ref.shape[0], :]


def unpack(g_ref, ny):
    width, nx = g_ref.shape
    return jnp.concatenate([g_ref[...], jnp.zeros((ny - width, nx), jnp.float32)], axis=0).T


def operator(q, west, east, below_ref, above_ref, c, vel_ref, visc_ref, snd_ref, coup_ref):
    nx, ny = q[0].shape
    rows = lax.broadcasted_iota(jnp.int32, (nx, ny), 0)
    lanes = lax.broadcasted_iota(jnp.int32, (nx, ny), 1)
    vel0 = vel_ref[0]
    vel1 = vel_ref[1]
    visc = visc_ref[...]
    snd = snd_ref[...]
    grad_x, grad_y, transport = [], [], []
    for v in range(NV):
        field = q[v]
        lo = 2 * NV * c + 2 * v
        north = pltpu.roll(above_ref[...], ny - 1 - lo, 1)
        south = pltpu.roll(below_ref[...], ny - 1 - lo, 1)
        e = jnp.where(rows == nx - 1, east[v], pltpu.roll(field, nx - 1, 0))
        w = jnp.where(rows == 0, west[v], pltpu.roll(field, 1, 0))
        n = jnp.where(lanes == ny - 1, north, pltpu.roll(field, ny - 1, 1))
        s = jnp.where(lanes == 0, south, pltpu.roll(field, 1, 1))
        gx = 0.5 * (e - w)
        gy = 0.5 * (n - s)
        laplace = e + w + n + s - 4.0 * field
        grad_x.append(gx)
        grad_y.append(gy)
        transport.append(visc * laplace - vel0 * gx - vel1 * gy)
    divergence = grad_x[1] + grad_y[2]
    acoustic = [-snd * divergence, -snd * grad_x[3], -snd * grad_y[3], -snd * divergence]
    out = []
    for w_ in range(NV):
        mixing = coup_ref[w_, 0] * q[0]
        for inner in range(1, NV):
            mixing = mixing + coup_ref[w_, inner] * q[inner]
        out.append(transport[w_] + acoustic[w_] - mixing)
    return out


def receive(c, gb_ref, ga_ref, below_ref, above_ref, ny):
    @pl.when(c == 0)
    def _():
        below_ref[...] = unpack(gb_ref, ny)
        above_ref[...] = unpack(ga_ref, ny)


def stage_one(f_ref, vel_ref, visc_ref, snd_ref, coup_ref, hw_ref, he_ref, gb_ref, ga_ref,
              first_ref, mid_ref, mw_ref, me_ref, g_ref, below_ref, above_ref, pack_ref):
    c = pl.program_id(0)
    nx, ny = f_ref.shape[2], f_ref.shape[3]
    receive(c, gb_ref, ga_ref, below_ref, above_ref, ny)
    q = [f_ref[v, 0] for v in range(NV)]
    west = [hw_ref[0, v:v + 1, :] for v in range(NV)]
    east = [he_ref[0, v:v + 1, :] for v in range(NV)]
    lq = operator(q, west, east, below_ref, above_ref, c, vel_ref, visc_ref, snd_ref, coup_ref)
    mids = []
    for v in range(NV):
        first = lq[v] + q[v]
        middle = q[v] + STEP * first
        first_ref[v, 0] = first
        mid_ref[v, 0] = middle
        mw_ref[0, v:v + 1, :] = middle[0:1, :]
        me_ref[0, v:v + 1, :] = middle[nx - 1:nx, :]
        mids.append(middle)
    pack(pack_ref, mids, c)

    @pl.when(c == pl.num_programs(0) - 1)
    def _():
        send_packed(pack_ref, g_ref)


def stage_two(f_ref, first_ref, mid_ref, vel_ref, visc_ref, snd_ref, coup_ref, hw_ref, he_ref, gb_ref, ga_ref,
              resp_ref, gram_ref, below_ref, above_ref):
    c = pl.program_id(0)
    ncol = resp_ref.shape[1]
    nx, ny = f_ref.shape[2], f_ref.shape[3]
    receive(c, gb_ref, ga_ref, below_ref, above_ref, ny)
    q = [mid_ref[v, 0] for v in range(NV)]
    west = [hw_ref[0, v:v + 1, :] for v in range(NV)]
    east = [he_ref[0, v:v + 1, :] for v in range(NV)]
    lq = operator(q, west, east, below_ref, above_ref, c, vel_ref, visc_ref, snd_ref, coup_ref)
    resp = []
    for v in range(NV):
        forcing = f_ref[v, 0]
        second = lq[v] + forcing
        r = forcing + 0.5 * STEP * (first_ref[v, 0] + second)
        resp_ref[v, pl.ds(c, 1)] = r[None]
        resp.append(r)
    for d in range(ncol):
        @pl.when(d <= c)
        def _():
            acc = None
            for v in range(NV):
                prod = (resp_ref[v, d] * resp[v]).reshape(nx // 8, 8, ny).sum(axis=0)
                acc = prod if acc is None else acc + prod
            row = jnp.sum(acc, axis=0, keepdims=True)
            gram_ref[pl.ds(c * ncol + d, 1), :] = row
            gram_ref[pl.ds(d * ncol + c, 1), :] = row


def edges(f_ref, w_ref, e_ref, g_ref, pack_ref):
    c = pl.program_id(0)
    nx = f_ref.shape[2]
    fields = [f_ref[v, 0] for v in range(NV)]
    for v in range(NV):
        w_ref[0, v:v + 1, :] = fields[v][0:1, :]
        e_ref[0, v:v + 1, :] = fields[v][nx - 1:nx, :]
    pack(pack_ref, fields, c)

    @pl.when(c == pl.num_programs(0) - 1)
    def _():
        send_packed(pack_ref, g_ref)


def combine(inv_ref, r_ref, out_ref):
    ncol = r_ref.shape[1]
    rs = [r_ref[0, d] for d in range(ncol)]
    for c in range(ncol):
        acc = inv_ref[c, 0] * rs[0]
        for d in range(1, ncol):
            acc = acc + inv_ref[c, d] * rs[d]
        out_ref[0, c] = acc


def local(forcing, velocity, viscosity, sound, coupling):
    nv, ncol, nx, ny = forcing.shape
    f32 = jnp.float32
    whole = lambda shape: pl.BlockSpec(shape, lambda c: (0,) * len(shape))
    column = pl.BlockSpec((nv, 1, nx, ny), lambda c: (0, c, 0, 0))
    edge_x = pl.BlockSpec((1, nv, ny), lambda c: (c, 0, 0))
    coef_specs = [whole((2, nx, ny)), whole((nx, ny)), whole((nx, ny)), whole((nv, nv, nx, ny))]
    params = pltpu.CompilerParams(vmem_limit_bytes=60 * 1024 * 1024)

    width = 2 * nv * ncol
    packed = whole((width, nx))
    packed_shape = jax.ShapeDtypeStruct((width, nx), f32)
    tile = pltpu.VMEM((nx, ny), f32)
    fw, fe, fg = pl.pallas_call(
        edges,
        grid=(ncol,),
        in_specs=[column],
        out_specs=[edge_x, edge_x, packed],
        out_shape=[
            jax.ShapeDtypeStruct((ncol, nv, ny), f32),
            jax.ShapeDtypeStruct((ncol, nv, ny), f32),
            packed_shape,
        ],
        scratch_shapes=[tile],
        compiler_params=params,
    )(forcing)
    hw, he = exchange(fw, fe, "gx")
    gb, ga = exchange(fg, fg, "gy")

    first, middle, mw, me, mg = pl.pallas_call(
        stage_one,
        grid=(ncol,),
        in_specs=[column] + coef_specs + [edge_x, edge_x, packed, packed],
        out_specs=[column, column, edge_x, edge_x, packed],
        out_shape=[
            jax.ShapeDtypeStruct(forcing.shape, f32),
            jax.ShapeDtypeStruct(forcing.shape, f32),
            jax.ShapeDtypeStruct((ncol, nv, ny), f32),
            jax.ShapeDtypeStruct((ncol, nv, ny), f32),
            packed_shape,
        ],
        scratch_shapes=[tile, tile, tile],
        compiler_params=params,
    )(forcing, velocity, viscosity, sound, coupling, hw, he, gb, ga)

    hw2, he2 = exchange(mw, me, "gx")
    gb2, ga2 = exchange(mg, mg, "gy")

    response, partial = pl.pallas_call(
        stage_two,
        grid=(ncol,),
        in_specs=[column, column, column] + coef_specs + [edge_x, edge_x, packed, packed],
        out_specs=[whole(forcing.shape), whole((ncol * ncol, ny))],
        out_shape=[
            jax.ShapeDtypeStruct(forcing.shape, f32),
            jax.ShapeDtypeStruct((ncol * ncol, ny), f32),
        ],
        compiler_params=pltpu.CompilerParams(
            vmem_limit_bytes=60 * 1024 * 1024, dimension_semantics=("arbitrary",)
        ),
        scratch_shapes=[tile, tile],
    )(forcing, first, middle, velocity, viscosity, sound, coupling, hw2, he2, gb2, ga2)

    rows_total = float(nv * nx * ny * lax.axis_size("gx") * lax.axis_size("gy"))
    local_gram = jnp.sum(partial, axis=1).reshape(ncol, ncol) / rows_total
    lower = jnp.linalg.cholesky(all_sum(local_gram))
    identity = jnp.eye(lower.shape[0], dtype=lower.dtype)
    inverse = lax.linalg.triangular_solve(lower, identity, left_side=True, lower=True)

    basis = pl.pallas_call(
        combine,
        grid=(nv,),
        in_specs=[
            pl.BlockSpec(memory_space=pltpu.SMEM),
            pl.BlockSpec((1, ncol, nx, ny), lambda v: (v, 0, 0, 0)),
        ],
        out_specs=pl.BlockSpec((1, ncol, nx, ny), lambda v: (v, 0, 0, 0)),
        out_shape=jax.ShapeDtypeStruct(forcing.shape, f32),
        compiler_params=params,
    )(inverse, response)
    return (basis, lower.T)


def solution(mesh):
    in_specs = (
        P(None, None, "gx", "gy"),
        P(None, "gx", "gy"),
        P("gx", "gy"),
        P("gx", "gy"),
        P(None, None, "gx", "gy"),
    )
    out_specs = (P(None, None, "gx", "gy"), P())
    return jax.shard_map(local, mesh=mesh, in_specs=in_specs, out_specs=out_specs, check_vma=False)
```

```python
import jax
import jax.numpy as jnp
from jax import lax
from jax.experimental import pallas as pl
from jax.experimental.pallas import tpu as pltpu
from jax.sharding import PartitionSpec as P

STEP = 0.5
NV = 4


def all_sum(value):
    for axis in ("gy", "gx"):
        count = lax.axis_size(axis)
        bit = 1
        while bit < count:
            value = value + lax.ppermute(value, axis, [(i, i ^ bit) for i in range(count)])
            bit *= 2
    return value


def exchange(low, high, axis):
    count = lax.axis_size(axis)
    from_below = lax.ppermute(high, axis, [(i, i + 1) for i in range(count - 1)])
    from_above = lax.ppermute(low, axis, [(i + 1, i) for i in range(count - 1)])
    return from_below, from_above


def pack(pack_ref, fields, c):
    nx, ny = fields[0].shape
    lanes = lax.broadcasted_iota(jnp.int32, (nx, ny), 1)
    cur = pack_ref[...]
    for v, field in enumerate(fields):
        lo = 2 * NV * c + 2 * v
        cur = jnp.where(lanes == lo, pltpu.roll(field, lo, 1), cur)
        cur = jnp.where(lanes == lo + 1, pltpu.roll(field, lo + 2, 1), cur)
    pack_ref[...] = cur


def send_packed(pack_ref, g_ref):
    g_ref[...] = pack_ref[...].T[0:g_ref.shape[0], :]


def unpack(g_ref, ny):
    width, nx = g_ref.shape
    return jnp.concatenate([g_ref[...], jnp.zeros((ny - width, nx), jnp.float32)], axis=0).T


def operator(q, west, east, below_ref, above_ref, c, vel_ref, visc_ref, snd_ref, coup_ref):
    nx, ny = q[0].shape
    rows = lax.broadcasted_iota(jnp.int32, (nx, ny), 0)
    lanes = lax.broadcasted_iota(jnp.int32, (nx, ny), 1)
    vel0 = vel_ref[0]
    vel1 = vel_ref[1]
    visc = visc_ref[...]
    snd = snd_ref[...]
    grad_x, grad_y, transport = [], [], []
    for v in range(NV):
        field = q[v]
        lo = 2 * NV * c + 2 * v
        north = pltpu.roll(above_ref[...], ny - 1 - lo, 1)
        south = pltpu.roll(below_ref[...], ny - 1 - lo, 1)
        e = jnp.where(rows == nx - 1, east[v], pltpu.roll(field, nx - 1, 0))
        w = jnp.where(rows == 0, west[v], pltpu.roll(field, 1, 0))
        n = jnp.where(lanes == ny - 1, north, pltpu.roll(field, ny - 1, 1))
        s = jnp.where(lanes == 0, south, pltpu.roll(field, 1, 1))
        gx = 0.5 * (e - w)
        gy = 0.5 * (n - s)
        laplace = e + w + n + s - 4.0 * field
        grad_x.append(gx)
        grad_y.append(gy)
        transport.append(visc * laplace - vel0 * gx - vel1 * gy)
    divergence = grad_x[1] + grad_y[2]
    acoustic = [-snd * divergence, -snd * grad_x[3], -snd * grad_y[3], -snd * divergence]
    out = []
    for w_ in range(NV):
        mixing = coup_ref[w_, 0] * q[0]
        for inner in range(1, NV):
            mixing = mixing + coup_ref[w_, inner] * q[inner]
        out.append(transport[w_] + acoustic[w_] - mixing)
    return out


def receive(c, gb_ref, ga_ref, below_ref, above_ref, ny):
    @pl.when(c == 0)
    def _():
        below_ref[...] = unpack(gb_ref, ny)
        above_ref[...] = unpack(ga_ref, ny)


def stage_one(f_ref, vel_ref, visc_ref, snd_ref, coup_ref, hw_ref, he_ref, gb_ref, ga_ref,
              first_ref, mid_ref, mw_ref, me_ref, g_ref, below_ref, above_ref, pack_ref):
    c = pl.program_id(0)
    nx, ny = f_ref.shape[2], f_ref.shape[3]
    receive(c, gb_ref, ga_ref, below_ref, above_ref, ny)
    q = [f_ref[v, 0] for v in range(NV)]
    west = [hw_ref[0, v:v + 1, :] for v in range(NV)]
    east = [he_ref[0, v:v + 1, :] for v in range(NV)]
    lq = operator(q, west, east, below_ref, above_ref, c, vel_ref, visc_ref, snd_ref, coup_ref)
    mids = []
    for v in range(NV):
        first = lq[v] + q[v]
        middle = q[v] + STEP * first
        first_ref[v, 0] = first
        mid_ref[v, 0] = middle
        mw_ref[0, v:v + 1, :] = middle[0:1, :]
        me_ref[0, v:v + 1, :] = middle[nx - 1:nx, :]
        mids.append(middle)
    pack(pack_ref, mids, c)

    @pl.when(c == pl.num_programs(0) - 1)
    def _():
        send_packed(pack_ref, g_ref)


def stage_two(f_ref, first_ref, mid_ref, vel_ref, visc_ref, snd_ref, coup_ref, hw_ref, he_ref, gb_ref, ga_ref,
              resp_ref, gram_ref, below_ref, above_ref):
    c = pl.program_id(0)
    ncol = resp_ref.shape[1]
    nx, ny = f_ref.shape[2], f_ref.shape[3]
    receive(c, gb_ref, ga_ref, below_ref, above_ref, ny)
    q = [mid_ref[v, 0] for v in range(NV)]
    west = [hw_ref[0, v:v + 1, :] for v in range(NV)]
    east = [he_ref[0, v:v + 1, :] for v in range(NV)]
    lq = operator(q, west, east, below_ref, above_ref, c, vel_ref, visc_ref, snd_ref, coup_ref)
    resp = []
    for v in range(NV):
        forcing = f_ref[v, 0]
        second = lq[v] + forcing
        r = forcing + 0.5 * STEP * (first_ref[v, 0] + second)
        resp_ref[v, pl.ds(c, 1)] = r[None]
        resp.append(r)
    for d in range(ncol):
        @pl.when(d <= c)
        def _():
            acc = None
            for v in range(NV):
                prod = (resp_ref[v, d] * resp[v]).reshape(nx // 8, 8, ny).sum(axis=0)
                acc = prod if acc is None else acc + prod
            row = jnp.sum(acc, axis=0, keepdims=True)
            gram_ref[pl.ds(c * ncol + d, 1), :] = row
            gram_ref[pl.ds(d * ncol + c, 1), :] = row


def edges(f_ref, w_ref, e_ref, g_ref, pack_ref):
    ncol, nx = f_ref.shape[1], f_ref.shape[2]
    for c in range(ncol):
        fields = [f_ref[v, c] for v in range(NV)]
        for v in range(NV):
            w_ref[c, v:v + 1, :] = fields[v][0:1, :]
            e_ref[c, v:v + 1, :] = fields[v][nx - 1:nx, :]
        pack(pack_ref, fields, c)
    send_packed(pack_ref, g_ref)


def combine(inv_ref, r_ref, out_ref):
    ncol = r_ref.shape[1]
    rs = [r_ref[0, d] for d in range(ncol)]
    for c in range(ncol):
        acc = inv_ref[c, 0] * rs[0]
        for d in range(1, ncol):
            acc = acc + inv_ref[c, d] * rs[d]
        out_ref[0, c] = acc


def local(forcing, velocity, viscosity, sound, coupling):
    nv, ncol, nx, ny = forcing.shape
    f32 = jnp.float32
    whole = lambda shape: pl.BlockSpec(shape, lambda c: (0,) * len(shape))
    column = pl.BlockSpec((nv, 1, nx, ny), lambda c: (0, c, 0, 0))
    edge_x = pl.BlockSpec((1, nv, ny), lambda c: (c, 0, 0))
    coef_specs = [whole((2, nx, ny)), whole((nx, ny)), whole((nx, ny)), whole((nv, nv, nx, ny))]
    params = pltpu.CompilerParams(vmem_limit_bytes=60 * 1024 * 1024)

    width = 2 * nv * ncol
    packed = whole((width, nx))
    packed_shape = jax.ShapeDtypeStruct((width, nx), f32)
    tile = pltpu.VMEM((nx, ny), f32)
    fw, fe, fg = pl.pallas_call(
        edges,
        in_specs=[pl.BlockSpec(memory_space=pltpu.VMEM)],
        out_specs=[pl.BlockSpec(memory_space=pltpu.VMEM)] * 3,
        out_shape=[
            jax.ShapeDtypeStruct((ncol, nv, ny), f32),
            jax.ShapeDtypeStruct((ncol, nv, ny), f32),
            packed_shape,
        ],
        scratch_shapes=[tile],
        compiler_params=params,
    )(forcing)
    hw, he = exchange(fw, fe, "gx")
    gb, ga = exchange(fg, fg, "gy")

    first, middle, mw, me, mg = pl.pallas_call(
        stage_one,
        grid=(ncol,),
        in_specs=[column] + coef_specs + [edge_x, edge_x, packed, packed],
        out_specs=[column, column, edge_x, edge_x, packed],
        out_shape=[
            jax.ShapeDtypeStruct(forcing.shape, f32),
            jax.ShapeDtypeStruct(forcing.shape, f32),
            jax.ShapeDtypeStruct((ncol, nv, ny), f32),
            jax.ShapeDtypeStruct((ncol, nv, ny), f32),
            packed_shape,
        ],
        scratch_shapes=[tile, tile, tile],
        compiler_params=params,
    )(forcing, velocity, viscosity, sound, coupling, hw, he, gb, ga)

    hw2, he2 = exchange(mw, me, "gx")
    gb2, ga2 = exchange(mg, mg, "gy")

    response, partial = pl.pallas_call(
        stage_two,
        grid=(ncol,),
        in_specs=[column, column, column] + coef_specs + [edge_x, edge_x, packed, packed],
        out_specs=[whole(forcing.shape), whole((ncol * ncol, ny))],
        out_shape=[
            jax.ShapeDtypeStruct(forcing.shape, f32),
            jax.ShapeDtypeStruct((ncol * ncol, ny), f32),
        ],
        compiler_params=pltpu.CompilerParams(
            vmem_limit_bytes=60 * 1024 * 1024, dimension_semantics=("arbitrary",)
        ),
        scratch_shapes=[tile, tile],
    )(forcing, first, middle, velocity, viscosity, sound, coupling, hw2, he2, gb2, ga2)

    rows_total = float(nv * nx * ny * lax.axis_size("gx") * lax.axis_size("gy"))
    local_gram = jnp.sum(partial, axis=1).reshape(ncol, ncol) / rows_total
    lower = jnp.linalg.cholesky(all_sum(local_gram))
    identity = jnp.eye(lower.shape[0], dtype=lower.dtype)
    inverse = lax.linalg.triangular_solve(lower, identity, left_side=True, lower=True)

    basis = pl.pallas_call(
        combine,
        grid=(nv,),
        in_specs=[
            pl.BlockSpec(memory_space=pltpu.SMEM),
            pl.BlockSpec((1, ncol, nx, ny), lambda v: (v, 0, 0, 0)),
        ],
        out_specs=pl.BlockSpec((1, ncol, nx, ny), lambda v: (v, 0, 0, 0)),
        out_shape=jax.ShapeDtypeStruct(forcing.shape, f32),
        compiler_params=params,
    )(inverse, response)
    return (basis, lower.T)


def solution(mesh):
    in_specs = (
        P(None, None, "gx", "gy"),
        P(None, "gx", "gy"),
        P("gx", "gy"),
        P("gx", "gy"),
        P(None, None, "gx", "gy"),
    )
    out_specs = (P(None, None, "gx", "gy"), P())
    return jax.shard_map(local, mesh=mesh, in_specs=in_specs, out_specs=out_specs, check_vma=False)
```

```python
import functools

import jax
import jax.numpy as jnp
from jax import lax
from jax.experimental import pallas as pl
from jax.experimental.pallas import tpu as pltpu
from jax.sharding import PartitionSpec as P

STEP = 0.5
NV = 4


def all_sum(value):
    for axis in ("gy", "gx"):
        count = lax.axis_size(axis)
        bit = 1
        while bit < count:
            value = value + lax.ppermute(value, axis, [(i, i ^ bit) for i in range(count)])
            bit *= 2
    return value


def exchange(low, high, axis):
    count = lax.axis_size(axis)
    from_below = lax.ppermute(high, axis, [(i, i + 1) for i in range(count - 1)])
    from_above = lax.ppermute(low, axis, [(i + 1, i) for i in range(count - 1)])
    return from_below, from_above


def pack(pack_ref, fields, c):
    nx, ny = fields[0].shape
    lanes = lax.broadcasted_iota(jnp.int32, (nx, ny), 1)
    cur = pack_ref[...]
    for v, field in enumerate(fields):
        lo = 2 * NV * c + 2 * v
        cur = jnp.where(lanes == lo, pltpu.roll(field, lo, 1), cur)
        cur = jnp.where(lanes == lo + 1, pltpu.roll(field, lo + 2, 1), cur)
    pack_ref[...] = cur


def send_packed(pack_ref, g_ref):
    g_ref[...] = pack_ref[...].T[0:g_ref.shape[0], :]


def unpack(g_ref, ny):
    width, nx = g_ref.shape
    return jnp.concatenate([g_ref[...], jnp.zeros((ny - width, nx), jnp.float32)], axis=0).T


def operator(q, west, east, below_ref, above_ref, c, vel_ref, visc_ref, snd_ref, coup_ref):
    nx, ny = q[0].shape
    rows = lax.broadcasted_iota(jnp.int32, (nx, ny), 0)
    lanes = lax.broadcasted_iota(jnp.int32, (nx, ny), 1)
    vel0 = vel_ref[0]
    vel1 = vel_ref[1]
    visc = visc_ref[...]
    snd = snd_ref[...]
    grad_x, grad_y, transport = [], [], []
    for v in range(NV):
        field = q[v]
        lo = 2 * NV * c + 2 * v
        north = pltpu.roll(above_ref[...], ny - 1 - lo, 1)
        south = pltpu.roll(below_ref[...], ny - 1 - lo, 1)
        e = jnp.where(rows == nx - 1, east[v], pltpu.roll(field, nx - 1, 0))
        w = jnp.where(rows == 0, west[v], pltpu.roll(field, 1, 0))
        n = jnp.where(lanes == ny - 1, north, pltpu.roll(field, ny - 1, 1))
        s = jnp.where(lanes == 0, south, pltpu.roll(field, 1, 1))
        gx = 0.5 * (e - w)
        gy = 0.5 * (n - s)
        laplace = e + w + n + s - 4.0 * field
        grad_x.append(gx)
        grad_y.append(gy)
        transport.append(visc * laplace - vel0 * gx - vel1 * gy)
    divergence = grad_x[1] + grad_y[2]
    acoustic = [-snd * divergence, -snd * grad_x[3], -snd * grad_y[3], -snd * divergence]
    out = []
    for w_ in range(NV):
        mixing = coup_ref[w_, 0] * q[0]
        for inner in range(1, NV):
            mixing = mixing + coup_ref[w_, inner] * q[inner]
        out.append(transport[w_] + acoustic[w_] - mixing)
    return out


def receive(c, gb_ref, ga_ref, below_ref, above_ref, ny):
    @pl.when(c == 0)
    def _():
        below_ref[...] = unpack(gb_ref, ny)
        above_ref[...] = unpack(ga_ref, ny)


def stage_one(f_ref, vel_ref, visc_ref, snd_ref, coup_ref, hw_ref, he_ref, gb_ref, ga_ref,
              first_ref, mid_ref, mw_ref, me_ref, g_ref, below_ref, above_ref, pack_ref):
    c = pl.program_id(0)
    nx, ny = f_ref.shape[2], f_ref.shape[3]
    receive(c, gb_ref, ga_ref, below_ref, above_ref, ny)
    q = [f_ref[v, 0] for v in range(NV)]
    west = [hw_ref[0, v:v + 1, :] for v in range(NV)]
    east = [he_ref[0, v:v + 1, :] for v in range(NV)]
    lq = operator(q, west, east, below_ref, above_ref, c, vel_ref, visc_ref, snd_ref, coup_ref)
    mids = []
    for v in range(NV):
        first = lq[v] + q[v]
        middle = q[v] + STEP * first
        first_ref[v, 0] = first
        mid_ref[v, 0] = middle
        mw_ref[0, v:v + 1, :] = middle[0:1, :]
        me_ref[0, v:v + 1, :] = middle[nx - 1:nx, :]
        mids.append(middle)
    pack(pack_ref, mids, c)

    @pl.when(c == pl.num_programs(0) - 1)
    def _():
        send_packed(pack_ref, g_ref)


def stage_two(c0, nprev, f_ref, first_ref, mid_ref, vel_ref, visc_ref, snd_ref, coup_ref, hw_ref, he_ref, gb_ref,
              ga_ref, *rest):
    prev_refs = rest[:nprev]
    resp_ref, gram_ref, below_ref, above_ref = rest[nprev:]
    c = pl.program_id(0)
    ncol = resp_ref.shape[1]
    total_cols = int(round(gram_ref.shape[0] ** 0.5))
    nx, ny = f_ref.shape[2], f_ref.shape[3]

    @pl.when(c == 0)
    def _():
        gram_ref[...] = jnp.zeros_like(gram_ref)

    receive(c, gb_ref, ga_ref, below_ref, above_ref, ny)
    q = [mid_ref[v, 0] for v in range(NV)]
    west = [hw_ref[0, v:v + 1, :] for v in range(NV)]
    east = [he_ref[0, v:v + 1, :] for v in range(NV)]
    lq = operator(q, west, east, below_ref, above_ref, c, vel_ref, visc_ref, snd_ref, coup_ref)
    resp = []
    for v in range(NV):
        forcing = f_ref[v, 0]
        second = lq[v] + forcing
        r = forcing + 0.5 * STEP * (first_ref[v, 0] + second)
        resp_ref[v, pl.ds(c, 1)] = r[None]
        resp.append(r)
    me = c0 + c

    def put(other, field_of):
        acc = None
        for v in range(NV):
            prod = (field_of(v) * resp[v]).reshape(nx // 8, 8, ny).sum(axis=0)
            acc = prod if acc is None else acc + prod
        row = jnp.sum(acc, axis=0, keepdims=True)
        gram_ref[pl.ds(me * total_cols + other, 1), :] = row
        gram_ref[pl.ds(other * total_cols + me, 1), :] = row

    base = 0
    for ref in prev_refs:
        for d in range(ref.shape[1]):
            put(base + d, lambda v, ref=ref, d=d: ref[v, d])
        base += ref.shape[1]
    for d in range(ncol):
        @pl.when(d <= c)
        def _():
            put(c0 + d, lambda v: resp_ref[v, d])


def edges(f_ref, w_ref, e_ref, g_ref, pack_ref):
    ncol, nx = w_ref.shape[0], f_ref.shape[2]
    for c in range(ncol):
        fields = [f_ref[v, c] for v in range(NV)]
        for v in range(NV):
            w_ref[c, v:v + 1, :] = fields[v][0:1, :]
            e_ref[c, v:v + 1, :] = fields[v][nx - 1:nx, :]
        pack(pack_ref, fields, c)
    send_packed(pack_ref, g_ref)


def combine(inv_ref, *refs):
    out_ref = refs[-1]
    rs = [r_ref[0, d] for r_ref in refs[:-1] for d in range(r_ref.shape[1])]
    ncol = len(rs)
    for c in range(ncol):
        acc = inv_ref[c, 0] * rs[0]
        for d in range(1, ncol):
            acc = acc + inv_ref[c, d] * rs[d]
        out_ref[0, c] = acc


def local(forcing, velocity, viscosity, sound, coupling):
    nv, ncol, nx, ny = forcing.shape
    groups = 2
    size = ncol // groups
    f32 = jnp.float32
    whole = lambda shape: pl.BlockSpec(shape, lambda c: (0,) * len(shape))
    coef_specs = [whole((2, nx, ny)), whole((nx, ny)), whole((nx, ny)), whole((nv, nv, nx, ny))]
    params = pltpu.CompilerParams(vmem_limit_bytes=60 * 1024 * 1024)
    width = 2 * nv * size
    packed = whole((width, nx))
    packed_shape = jax.ShapeDtypeStruct((width, nx), f32)
    tile = pltpu.VMEM((nx, ny), f32)
    edge_x = pl.BlockSpec((1, nv, ny), lambda c: (c, 0, 0))
    local_col = pl.BlockSpec((nv, 1, nx, ny), lambda c: (0, c, 0, 0))
    group_shape = jax.ShapeDtypeStruct((nv, size, nx, ny), f32)
    edge_shape = jax.ShapeDtypeStruct((size, nv, ny), f32)

    responses, partials = [], []
    for g in range(groups):
        c0 = g * size
        global_col = pl.BlockSpec((nv, 1, nx, ny), lambda c, c0=c0: (0, c + c0, 0, 0))
        fw, fe, fg = pl.pallas_call(
            edges,
            grid=(1,),
            in_specs=[pl.BlockSpec((nv, size, nx, ny), lambda i, g=g: (0, g, 0, 0))],
            out_specs=[whole((size, nv, ny)), whole((size, nv, ny)), packed],
            out_shape=[edge_shape, edge_shape, packed_shape],
            scratch_shapes=[tile],
            compiler_params=params,
        )(forcing)
        hw, he = exchange(fw, fe, "gx")
        gb, ga = exchange(fg, fg, "gy")

        first, middle, mw, me, mg = pl.pallas_call(
            stage_one,
            grid=(size,),
            in_specs=[global_col] + coef_specs + [edge_x, edge_x, packed, packed],
            out_specs=[local_col, local_col, edge_x, edge_x, packed],
            out_shape=[group_shape, group_shape, edge_shape, edge_shape, packed_shape],
            scratch_shapes=[tile, tile, tile],
            compiler_params=params,
        )(forcing, velocity, viscosity, sound, coupling, hw, he, gb, ga)

        hw2, he2 = exchange(mw, me, "gx")
        gb2, ga2 = exchange(mg, mg, "gy")

        response, partial = pl.pallas_call(
            functools.partial(stage_two, c0, len(responses)),
            grid=(size,),
            in_specs=[global_col, local_col, local_col] + coef_specs + [edge_x, edge_x, packed, packed]
            + [whole((nv, size, nx, ny))] * len(responses),
            out_specs=[whole((nv, size, nx, ny)), whole((ncol * ncol, ny))],
            out_shape=[group_shape, jax.ShapeDtypeStruct((ncol * ncol, ny), f32)],
            compiler_params=pltpu.CompilerParams(
                vmem_limit_bytes=60 * 1024 * 1024, dimension_semantics=("arbitrary",)
            ),
            scratch_shapes=[tile, tile],
        )(forcing, first, middle, velocity, viscosity, sound, coupling, hw2, he2, gb2, ga2, *responses)
        responses.append(response)
        partials.append(partial)

    rows_total = float(nv * nx * ny * lax.axis_size("gx") * lax.axis_size("gy"))
    partial = partials[0]
    for more in partials[1:]:
        partial = partial + more
    local_gram = jnp.sum(partial, axis=1).reshape(ncol, ncol) / rows_total
    lower = jnp.linalg.cholesky(all_sum(local_gram))
    identity = jnp.eye(lower.shape[0], dtype=lower.dtype)
    inverse = lax.linalg.triangular_solve(lower, identity, left_side=True, lower=True)

    basis = pl.pallas_call(
        combine,
        grid=(nv,),
        in_specs=[pl.BlockSpec(memory_space=pltpu.SMEM)]
        + [pl.BlockSpec((1, size, nx, ny), lambda v: (v, 0, 0, 0))] * groups,
        out_specs=pl.BlockSpec((1, ncol, nx, ny), lambda v: (v, 0, 0, 0)),
        out_shape=jax.ShapeDtypeStruct(forcing.shape, f32),
        compiler_params=params,
    )(inverse, *responses)
    return (basis, lower.T)


def solution(mesh):
    in_specs = (
        P(None, None, "gx", "gy"),
        P(None, "gx", "gy"),
        P("gx", "gy"),
        P("gx", "gy"),
        P(None, None, "gx", "gy"),
    )
    out_specs = (P(None, None, "gx", "gy"), P())
    return jax.shard_map(local, mesh=mesh, in_specs=in_specs, out_specs=out_specs, check_vma=False)
```

```python
import jax
import jax.numpy as jnp
from jax import lax
from jax.experimental import pallas as pl
from jax.experimental.pallas import tpu as pltpu
from jax.sharding import PartitionSpec as P

STEP = 0.5
NV = 4


def all_sum(value):
    for axis in ("gy", "gx"):
        count = lax.axis_size(axis)
        bit = 1
        while bit < count:
            value = value + lax.ppermute(value, axis, [(i, i ^ bit) for i in range(count)])
            bit *= 2
    return value


def exchange(low, high, axis):
    count = lax.axis_size(axis)
    from_below = lax.ppermute(high, axis, [(i, i + 1) for i in range(count - 1)])
    from_above = lax.ppermute(low, axis, [(i + 1, i) for i in range(count - 1)])
    return from_below, from_above


def pack(pack_ref, fields, c):
    nx, ny = fields[0].shape
    lanes = lax.broadcasted_iota(jnp.int32, (nx, ny), 1)
    cur = pack_ref[...]
    for v, field in enumerate(fields):
        lo = 2 * NV * c + 2 * v
        cur = jnp.where(lanes == lo, pltpu.roll(field, lo, 1), cur)
        cur = jnp.where(lanes == lo + 1, pltpu.roll(field, lo + 2, 1), cur)
    pack_ref[...] = cur


def send_packed(pack_ref, g_ref):
    g_ref[...] = pack_ref[...].T[0:g_ref.shape[0], :]


def unpack(g_ref, ny):
    width, nx = g_ref.shape
    return jnp.concatenate([g_ref[...], jnp.zeros((ny - width, nx), jnp.float32)], axis=0).T


def operator(q, west, east, below_ref, above_ref, c, vel_ref, visc_ref, snd_ref, coup_ref):
    nx, ny = q[0].shape
    rows = lax.broadcasted_iota(jnp.int32, (nx, ny), 0)
    lanes = lax.broadcasted_iota(jnp.int32, (nx, ny), 1)
    vel0 = vel_ref[0]
    vel1 = vel_ref[1]
    visc = visc_ref[...]
    snd = snd_ref[...]
    grad_x, grad_y, transport = [], [], []
    for v in range(NV):
        field = q[v]
        lo = 2 * NV * c + 2 * v
        north = pltpu.roll(above_ref[...], ny - 1 - lo, 1)
        south = pltpu.roll(below_ref[...], ny - 1 - lo, 1)
        e = jnp.where(rows == nx - 1, east[v], pltpu.roll(field, nx - 1, 0))
        w = jnp.where(rows == 0, west[v], pltpu.roll(field, 1, 0))
        n = jnp.where(lanes == ny - 1, north, pltpu.roll(field, ny - 1, 1))
        s = jnp.where(lanes == 0, south, pltpu.roll(field, 1, 1))
        gx = 0.5 * (e - w)
        gy = 0.5 * (n - s)
        laplace = e + w + n + s - 4.0 * field
        grad_x.append(gx)
        grad_y.append(gy)
        transport.append(visc * laplace - vel0 * gx - vel1 * gy)
    divergence = grad_x[1] + grad_y[2]
    acoustic = [-snd * divergence, -snd * grad_x[3], -snd * grad_y[3], -snd * divergence]
    out = []
    for w_ in range(NV):
        mixing = coup_ref[w_, 0] * q[0]
        for inner in range(1, NV):
            mixing = mixing + coup_ref[w_, inner] * q[inner]
        out.append(transport[w_] + acoustic[w_] - mixing)
    return out


def receive(c, gb_ref, ga_ref, below_ref, above_ref, ny):
    @pl.when(c == 0)
    def _():
        below_ref[...] = unpack(gb_ref, ny)
        above_ref[...] = unpack(ga_ref, ny)


def stage_one(f_ref, vel_ref, visc_ref, snd_ref, coup_ref, hw_ref, he_ref, gb_ref, ga_ref,
              first_ref, mw_ref, me_ref, g_ref, below_ref, above_ref, pack_ref):
    c = pl.program_id(0)
    nx, ny = f_ref.shape[2], f_ref.shape[3]
    receive(c, gb_ref, ga_ref, below_ref, above_ref, ny)
    q = [f_ref[v, 0] for v in range(NV)]
    west = [hw_ref[0, v:v + 1, :] for v in range(NV)]
    east = [he_ref[0, v:v + 1, :] for v in range(NV)]
    lq = operator(q, west, east, below_ref, above_ref, c, vel_ref, visc_ref, snd_ref, coup_ref)
    mids = []
    for v in range(NV):
        first = lq[v] + q[v]
        middle = q[v] + STEP * first
        first_ref[v, 0] = first
        mw_ref[0, v:v + 1, :] = middle[0:1, :]
        me_ref[0, v:v + 1, :] = middle[nx - 1:nx, :]
        mids.append(middle)
    pack(pack_ref, mids, c)

    @pl.when(c == pl.num_programs(0) - 1)
    def _():
        send_packed(pack_ref, g_ref)


def stage_two(f_ref, first_ref, vel_ref, visc_ref, snd_ref, coup_ref, hw_ref, he_ref, gb_ref, ga_ref,
              resp_ref, gram_ref, below_ref, above_ref):
    c = pl.program_id(0)
    ncol = resp_ref.shape[1]
    nx, ny = f_ref.shape[2], f_ref.shape[3]
    receive(c, gb_ref, ga_ref, below_ref, above_ref, ny)
    q = [f_ref[v, 0] + STEP * first_ref[v, 0] for v in range(NV)]
    west = [hw_ref[0, v:v + 1, :] for v in range(NV)]
    east = [he_ref[0, v:v + 1, :] for v in range(NV)]
    lq = operator(q, west, east, below_ref, above_ref, c, vel_ref, visc_ref, snd_ref, coup_ref)
    resp = []
    for v in range(NV):
        forcing = f_ref[v, 0]
        second = lq[v] + forcing
        r = forcing + 0.5 * STEP * (first_ref[v, 0] + second)
        resp_ref[v, pl.ds(c, 1)] = r[None]
        resp.append(r)
    for d in range(ncol):
        @pl.when(d <= c)
        def _():
            acc = None
            for v in range(NV):
                prod = (resp_ref[v, d] * resp[v]).reshape(nx // 8, 8, ny).sum(axis=0)
                acc = prod if acc is None else acc + prod
            row = jnp.sum(acc, axis=0, keepdims=True)
            gram_ref[pl.ds(c * ncol + d, 1), :] = row
            gram_ref[pl.ds(d * ncol + c, 1), :] = row


def edges(f_ref, w_ref, e_ref, g_ref, pack_ref):
    ncol, nx = f_ref.shape[1], f_ref.shape[2]
    for c in range(ncol):
        fields = [f_ref[v, c] for v in range(NV)]
        for v in range(NV):
            w_ref[c, v:v + 1, :] = fields[v][0:1, :]
            e_ref[c, v:v + 1, :] = fields[v][nx - 1:nx, :]
        pack(pack_ref, fields, c)
    send_packed(pack_ref, g_ref)


def combine(inv_ref, r_ref, out_ref):
    ncol = r_ref.shape[1]
    rs = [r_ref[0, d] for d in range(ncol)]
    for c in range(ncol):
        acc = inv_ref[c, 0] * rs[0]
        for d in range(1, ncol):
            acc = acc + inv_ref[c, d] * rs[d]
        out_ref[0, c] = acc


def local(forcing, velocity, viscosity, sound, coupling):
    nv, ncol, nx, ny = forcing.shape
    f32 = jnp.float32
    whole = lambda shape: pl.BlockSpec(shape, lambda c: (0,) * len(shape))
    column = pl.BlockSpec((nv, 1, nx, ny), lambda c: (0, c, 0, 0))
    edge_x = pl.BlockSpec((1, nv, ny), lambda c: (c, 0, 0))
    coef_specs = [whole((2, nx, ny)), whole((nx, ny)), whole((nx, ny)), whole((nv, nv, nx, ny))]
    params = pltpu.CompilerParams(vmem_limit_bytes=60 * 1024 * 1024)

    width = 2 * nv * ncol
    packed = whole((width, nx))
    packed_shape = jax.ShapeDtypeStruct((width, nx), f32)
    tile = pltpu.VMEM((nx, ny), f32)
    fw, fe, fg = pl.pallas_call(
        edges,
        in_specs=[pl.BlockSpec(memory_space=pltpu.VMEM)],
        out_specs=[pl.BlockSpec(memory_space=pltpu.VMEM)] * 3,
        out_shape=[
            jax.ShapeDtypeStruct((ncol, nv, ny), f32),
            jax.ShapeDtypeStruct((ncol, nv, ny), f32),
            packed_shape,
        ],
        scratch_shapes=[tile],
        compiler_params=params,
    )(forcing)
    hw, he = exchange(fw, fe, "gx")
    gb, ga = exchange(fg, fg, "gy")

    first, mw, me, mg = pl.pallas_call(
        stage_one,
        grid=(ncol,),
        in_specs=[column] + coef_specs + [edge_x, edge_x, packed, packed],
        out_specs=[column, edge_x, edge_x, packed],
        out_shape=[
            jax.ShapeDtypeStruct(forcing.shape, f32),
            jax.ShapeDtypeStruct((ncol, nv, ny), f32),
            jax.ShapeDtypeStruct((ncol, nv, ny), f32),
            packed_shape,
        ],
        scratch_shapes=[tile, tile, tile],
        compiler_params=params,
    )(forcing, velocity, viscosity, sound, coupling, hw, he, gb, ga)

    hw2, he2 = exchange(mw, me, "gx")
    gb2, ga2 = exchange(mg, mg, "gy")

    response, partial = pl.pallas_call(
        stage_two,
        grid=(ncol,),
        in_specs=[column, column] + coef_specs + [edge_x, edge_x, packed, packed],
        out_specs=[whole(forcing.shape), whole((ncol * ncol, ny))],
        out_shape=[
            jax.ShapeDtypeStruct(forcing.shape, f32),
            jax.ShapeDtypeStruct((ncol * ncol, ny), f32),
        ],
        compiler_params=pltpu.CompilerParams(
            vmem_limit_bytes=60 * 1024 * 1024, dimension_semantics=("arbitrary",)
        ),
        scratch_shapes=[tile, tile],
    )(forcing, first, velocity, viscosity, sound, coupling, hw2, he2, gb2, ga2)

    rows_total = float(nv * nx * ny * lax.axis_size("gx") * lax.axis_size("gy"))
    local_gram = jnp.sum(partial, axis=1).reshape(ncol, ncol) / rows_total
    lower = jnp.linalg.cholesky(all_sum(local_gram))
    identity = jnp.eye(lower.shape[0], dtype=lower.dtype)
    inverse = lax.linalg.triangular_solve(lower, identity, left_side=True, lower=True)

    basis = pl.pallas_call(
        combine,
        grid=(nv, 2),
        in_specs=[
            pl.BlockSpec(memory_space=pltpu.SMEM),
            pl.BlockSpec((1, ncol, nx // 2, ny), lambda v, h: (v, 0, h, 0)),
        ],
        out_specs=pl.BlockSpec((1, ncol, nx // 2, ny), lambda v, h: (v, 0, h, 0)),
        out_shape=jax.ShapeDtypeStruct(forcing.shape, f32),
        compiler_params=params,
    )(inverse, response)
    return (basis, lower.T)


def solution(mesh):
    in_specs = (
        P(None, None, "gx", "gy"),
        P(None, "gx", "gy"),
        P("gx", "gy"),
        P("gx", "gy"),
        P(None, None, "gx", "gy"),
    )
    out_specs = (P(None, None, "gx", "gy"), P())
    return jax.shard_map(local, mesh=mesh, in_specs=in_specs, out_specs=out_specs, check_vma=False)
```

```python
import jax
import jax.numpy as jnp
from jax import lax
from jax.experimental import pallas as pl
from jax.experimental.pallas import tpu as pltpu
from jax.sharding import PartitionSpec as P

STEP = 0.5
NV = 4


def all_sum(value):
    for axis in ("gy", "gx"):
        count = lax.axis_size(axis)
        bit = 1
        while bit < count:
            value = value + lax.ppermute(value, axis, [(i, i ^ bit) for i in range(count)])
            bit *= 2
    return value


def exchange(low, high, axis):
    count = lax.axis_size(axis)
    from_below = lax.ppermute(high, axis, [(i, i + 1) for i in range(count - 1)])
    from_above = lax.ppermute(low, axis, [(i + 1, i) for i in range(count - 1)])
    return from_below, from_above


def pack(pack_ref, fields, c):
    nx, ny = fields[0].shape
    lanes = lax.broadcasted_iota(jnp.int32, (nx, ny), 1)
    cur = pack_ref[...]
    for v, field in enumerate(fields):
        lo = 2 * NV * c + 2 * v
        cur = jnp.where(lanes == lo, pltpu.roll(field, lo, 1), cur)
        cur = jnp.where(lanes == lo + 1, pltpu.roll(field, lo + 2, 1), cur)
    pack_ref[...] = cur


def send_packed(pack_ref, g_ref):
    g_ref[...] = pack_ref[...].T[0:g_ref.shape[0], :]


def unpack(g_ref, ny):
    width, nx = g_ref.shape
    return jnp.concatenate([g_ref[...], jnp.zeros((ny - width, nx), jnp.float32)], axis=0).T


def operator(q, west, east, below_ref, above_ref, c, vel_ref, visc_ref, snd_ref, coup_ref):
    nx, ny = q[0].shape
    rows = lax.broadcasted_iota(jnp.int32, (nx, ny), 0)
    lanes = lax.broadcasted_iota(jnp.int32, (nx, ny), 1)
    vel0 = vel_ref[0]
    vel1 = vel_ref[1]
    visc = visc_ref[...]
    snd = snd_ref[...]
    grad_x, grad_y, transport = [], [], []
    for v in range(NV):
        field = q[v]
        lo = 2 * NV * c + 2 * v
        north = pltpu.roll(above_ref[...], ny - 1 - lo, 1)
        south = pltpu.roll(below_ref[...], ny - 1 - lo, 1)
        e = jnp.where(rows == nx - 1, east[v], pltpu.roll(field, nx - 1, 0))
        w = jnp.where(rows == 0, west[v], pltpu.roll(field, 1, 0))
        n = jnp.where(lanes == ny - 1, north, pltpu.roll(field, ny - 1, 1))
        s = jnp.where(lanes == 0, south, pltpu.roll(field, 1, 1))
        gx = 0.5 * (e - w)
        gy = 0.5 * (n - s)
        laplace = e + w + n + s - 4.0 * field
        grad_x.append(gx)
        grad_y.append(gy)
        transport.append(visc * laplace - vel0 * gx - vel1 * gy)
    divergence = grad_x[1] + grad_y[2]
    acoustic = [-snd * divergence, -snd * grad_x[3], -snd * grad_y[3], -snd * divergence]
    out = []
    for w_ in range(NV):
        mixing = coup_ref[w_, 0] * q[0]
        for inner in range(1, NV):
            mixing = mixing + coup_ref[w_, inner] * q[inner]
        out.append(transport[w_] + acoustic[w_] - mixing)
    return out


def receive(c, gb_ref, ga_ref, below_ref, above_ref, ny):
    @pl.when(c == 0)
    def _():
        below_ref[...] = unpack(gb_ref, ny)
        above_ref[...] = unpack(ga_ref, ny)


def stage_one(f_ref, vel_ref, visc_ref, snd_ref, coup_ref, hw_ref, he_ref, gb_ref, ga_ref,
              first_ref, mw_ref, me_ref, g_ref, below_ref, above_ref, pack_ref):
    c = pl.program_id(0)
    nx, ny = f_ref.shape[2], f_ref.shape[3]
    receive(c, gb_ref, ga_ref, below_ref, above_ref, ny)
    q = [f_ref[v, 0] for v in range(NV)]
    west = [hw_ref[0, v:v + 1, :] for v in range(NV)]
    east = [he_ref[0, v:v + 1, :] for v in range(NV)]
    lq = operator(q, west, east, below_ref, above_ref, c, vel_ref, visc_ref, snd_ref, coup_ref)
    mids = []
    for v in range(NV):
        first = lq[v] + q[v]
        middle = q[v] + STEP * first
        first_ref[v, 0] = first
        mw_ref[0, v:v + 1, :] = middle[0:1, :]
        me_ref[0, v:v + 1, :] = middle[nx - 1:nx, :]
        mids.append(middle)
    pack(pack_ref, mids, c)

    @pl.when(c == pl.num_programs(0) - 1)
    def _():
        send_packed(pack_ref, g_ref)


def stage_two(f_ref, first_ref, vel_ref, visc_ref, snd_ref, coup_ref, hw_ref, he_ref, gb_ref, ga_ref,
              resp_ref, gram_ref, below_ref, above_ref):
    c = pl.program_id(0)
    ncol = resp_ref.shape[1]
    nx, ny = f_ref.shape[2], f_ref.shape[3]
    receive(c, gb_ref, ga_ref, below_ref, above_ref, ny)
    q = [f_ref[v, 0] + STEP * first_ref[v, 0] for v in range(NV)]
    west = [hw_ref[0, v:v + 1, :] for v in range(NV)]
    east = [he_ref[0, v:v + 1, :] for v in range(NV)]
    lq = operator(q, west, east, below_ref, above_ref, c, vel_ref, visc_ref, snd_ref, coup_ref)
    resp = []
    for v in range(NV):
        forcing = f_ref[v, 0]
        second = lq[v] + forcing
        r = forcing + 0.5 * STEP * (first_ref[v, 0] + second)
        resp_ref[v, pl.ds(c, 1)] = r[None]
        resp.append(r)
    for d in range(ncol):
        @pl.when(d <= c)
        def _():
            acc = None
            for v in range(NV):
                prod = (resp_ref[v, d] * resp[v]).reshape(nx // 8, 8, ny).sum(axis=0)
                acc = prod if acc is None else acc + prod
            row = jnp.sum(acc, axis=0, keepdims=True)
            gram_ref[pl.ds(c * ncol + d, 1), :] = row
            gram_ref[pl.ds(d * ncol + c, 1), :] = row


def edges(f_ref, w_ref, e_ref, g_ref, pack_ref):
    ncol, nx = f_ref.shape[1], f_ref.shape[2]
    for c in range(ncol):
        fields = [f_ref[v, c] for v in range(NV)]
        for v in range(NV):
            w_ref[c, v:v + 1, :] = fields[v][0:1, :]
            e_ref[c, v:v + 1, :] = fields[v][nx - 1:nx, :]
        pack(pack_ref, fields, c)
    send_packed(pack_ref, g_ref)


def combine(inv_ref, r_ref, out_ref):
    ncol = r_ref.shape[1]
    rs = [r_ref[0, d] for d in range(ncol)]
    for c in range(ncol):
        acc = inv_ref[c, 0] * rs[0]
        for d in range(1, ncol):
            acc = acc + inv_ref[c, d] * rs[d]
        out_ref[0, c] = acc


def local(forcing, velocity, viscosity, sound, coupling):
    nv, ncol, nx, ny = forcing.shape
    f32 = jnp.float32
    whole = lambda shape: pl.BlockSpec(shape, lambda c: (0,) * len(shape))
    column = pl.BlockSpec((nv, 1, nx, ny), lambda c: (0, c, 0, 0))
    edge_x = pl.BlockSpec((1, nv, ny), lambda c: (c, 0, 0))
    coef_specs = [whole((2, nx, ny)), whole((nx, ny)), whole((nx, ny)), whole((nv, nv, nx, ny))]
    params = pltpu.CompilerParams(vmem_limit_bytes=60 * 1024 * 1024)

    width = 2 * nv * ncol
    packed = whole((width, nx))
    packed_shape = jax.ShapeDtypeStruct((width, nx), f32)
    tile = pltpu.VMEM((nx, ny), f32)
    fw, fe, fg = pl.pallas_call(
        edges,
        in_specs=[pl.BlockSpec(memory_space=pltpu.VMEM)],
        out_specs=[pl.BlockSpec(memory_space=pltpu.VMEM)] * 3,
        out_shape=[
            jax.ShapeDtypeStruct((ncol, nv, ny), f32),
            jax.ShapeDtypeStruct((ncol, nv, ny), f32),
            packed_shape,
        ],
        scratch_shapes=[tile],
        compiler_params=params,
    )(forcing)
    hw, he = exchange(fw, fe, "gx")
    gb, ga = exchange(fg, fg, "gy")

    first, mw, me, mg = pl.pallas_call(
        stage_one,
        grid=(ncol,),
        in_specs=[column] + coef_specs + [edge_x, edge_x, packed, packed],
        out_specs=[column, edge_x, edge_x, packed],
        out_shape=[
            jax.ShapeDtypeStruct(forcing.shape, f32),
            jax.ShapeDtypeStruct((ncol, nv, ny), f32),
            jax.ShapeDtypeStruct((ncol, nv, ny), f32),
            packed_shape,
        ],
        scratch_shapes=[tile, tile, tile],
        compiler_params=params,
    )(forcing, velocity, viscosity, sound, coupling, hw, he, gb, ga)

    hw2, he2 = exchange(mw, me, "gx")
    gb2, ga2 = exchange(mg, mg, "gy")

    response, partial = pl.pallas_call(
        stage_two,
        grid=(ncol,),
        in_specs=[column, column] + coef_specs + [edge_x, edge_x, packed, packed],
        out_specs=[whole(forcing.shape), whole((ncol * ncol, ny))],
        out_shape=[
            jax.ShapeDtypeStruct(forcing.shape, f32),
            jax.ShapeDtypeStruct((ncol * ncol, ny), f32),
        ],
        compiler_params=pltpu.CompilerParams(
            vmem_limit_bytes=60 * 1024 * 1024, dimension_semantics=("arbitrary",)
        ),
        scratch_shapes=[tile, tile],
    )(forcing, first, velocity, viscosity, sound, coupling, hw2, he2, gb2, ga2)

    rows_total = float(nv * nx * ny * lax.axis_size("gx") * lax.axis_size("gy"))
    local_gram = jnp.sum(partial, axis=1).reshape(ncol, ncol) / rows_total
    lower = jnp.linalg.cholesky(all_sum(local_gram))
    identity = jnp.eye(lower.shape[0], dtype=lower.dtype)
    inverse = lax.linalg.triangular_solve(lower, identity, left_side=True, lower=True)

    basis = pl.pallas_call(
        combine,
        grid=(nv,),
        in_specs=[
            pl.BlockSpec(memory_space=pltpu.SMEM),
            pl.BlockSpec((1, ncol, nx, ny), lambda v: (v, 0, 0, 0)),
        ],
        out_specs=pl.BlockSpec((1, ncol, nx, ny), lambda v: (v, 0, 0, 0)),
        out_shape=jax.ShapeDtypeStruct(forcing.shape, f32),
        compiler_params=params,
    )(inverse, response)
    return (basis, lower.T)


def solution(mesh):
    in_specs = (
        P(None, None, "gx", "gy"),
        P(None, "gx", "gy"),
        P("gx", "gy"),
        P("gx", "gy"),
        P(None, None, "gx", "gy"),
    )
    out_specs = (P(None, None, "gx", "gy"), P())
    return jax.shard_map(local, mesh=mesh, in_specs=in_specs, out_specs=out_specs, check_vma=False)
```

```python
import jax
import jax.numpy as jnp
from jax import lax
from jax.experimental import pallas as pl
from jax.experimental.pallas import tpu as pltpu
from jax.sharding import PartitionSpec as P

STEP = 0.5
NV = 4


def all_sum(value):
    for axis in ("gy", "gx"):
        count = lax.axis_size(axis)
        bit = 1
        while bit < count:
            value = value + lax.ppermute(value, axis, [(i, i ^ bit) for i in range(count)])
            bit *= 2
    return value


def exchange(low, high, axis):
    count = lax.axis_size(axis)
    from_below = lax.ppermute(high, axis, [(i, i + 1) for i in range(count - 1)])
    from_above = lax.ppermute(low, axis, [(i + 1, i) for i in range(count - 1)])
    return from_below, from_above


def pack(pack_ref, fields, c):
    nx, ny = fields[0].shape
    lanes = lax.broadcasted_iota(jnp.int32, (nx, ny), 1)
    cur = pack_ref[...]
    for v, field in enumerate(fields):
        lo = 2 * NV * c + 2 * v
        cur = jnp.where(lanes == lo, pltpu.roll(field, lo, 1), cur)
        cur = jnp.where(lanes == lo + 1, pltpu.roll(field, lo + 2, 1), cur)
    pack_ref[...] = cur


def send_packed(pack_ref, g_ref):
    g_ref[...] = pack_ref[...].T[0:g_ref.shape[0], :]


def unpack(g_ref, ny):
    width, nx = g_ref.shape
    return jnp.concatenate([g_ref[...], jnp.zeros((ny - width, nx), jnp.float32)], axis=0).T


def operator(q, west, east, below_ref, above_ref, c, vel_ref, visc_ref, snd_ref, coup_ref):
    nx, ny = q[0].shape
    slab = lax.broadcasted_iota(jnp.int32, (8, ny), 0)
    lanes = lax.broadcasted_iota(jnp.int32, (nx, ny), 1)
    vel0 = vel_ref[0]
    vel1 = vel_ref[1]
    visc = visc_ref[...]
    snd = snd_ref[...]
    grad_x, grad_y, transport = [], [], []
    for v in range(NV):
        field = q[v]
        lo = 2 * NV * c + 2 * v
        north = pltpu.roll(above_ref[...], ny - 1 - lo, 1)
        south = pltpu.roll(below_ref[...], ny - 1 - lo, 1)
        e = pltpu.roll(field, nx - 1, 0)
        e = jnp.concatenate([e[:nx - 8], jnp.where(slab == 7, east[v], e[nx - 8:])], axis=0)
        w = pltpu.roll(field, 1, 0)
        w = jnp.concatenate([jnp.where(slab == 0, west[v], w[:8]), w[8:]], axis=0)
        n = jnp.where(lanes == ny - 1, north, pltpu.roll(field, ny - 1, 1))
        s = jnp.where(lanes == 0, south, pltpu.roll(field, 1, 1))
        gx = 0.5 * (e - w)
        gy = 0.5 * (n - s)
        laplace = e + w + n + s - 4.0 * field
        grad_x.append(gx)
        grad_y.append(gy)
        transport.append(visc * laplace - vel0 * gx - vel1 * gy)
    divergence = grad_x[1] + grad_y[2]
    acoustic = [-snd * divergence, -snd * grad_x[3], -snd * grad_y[3], -snd * divergence]
    out = []
    for w_ in range(NV):
        mixing = coup_ref[w_, 0] * q[0]
        for inner in range(1, NV):
            mixing = mixing + coup_ref[w_, inner] * q[inner]
        out.append(transport[w_] + acoustic[w_] - mixing)
    return out


def receive(c, gb_ref, ga_ref, below_ref, above_ref, ny):
    @pl.when(c == 0)
    def _():
        below_ref[...] = unpack(gb_ref, ny)
        above_ref[...] = unpack(ga_ref, ny)


def stage_one(f_ref, vel_ref, visc_ref, snd_ref, coup_ref, hw_ref, he_ref, gb_ref, ga_ref,
              first_ref, mw_ref, me_ref, g_ref, below_ref, above_ref, pack_ref):
    c = pl.program_id(0)
    nx, ny = f_ref.shape[2], f_ref.shape[3]
    receive(c, gb_ref, ga_ref, below_ref, above_ref, ny)
    q = [f_ref[v, 0] for v in range(NV)]
    west = [hw_ref[0, v:v + 1, :] for v in range(NV)]
    east = [he_ref[0, v:v + 1, :] for v in range(NV)]
    lq = operator(q, west, east, below_ref, above_ref, c, vel_ref, visc_ref, snd_ref, coup_ref)
    mids = []
    for v in range(NV):
        first = lq[v] + q[v]
        middle = q[v] + STEP * first
        first_ref[v, 0] = first
        mw_ref[0, v:v + 1, :] = middle[0:1, :]
        me_ref[0, v:v + 1, :] = middle[nx - 1:nx, :]
        mids.append(middle)
    pack(pack_ref, mids, c)

    @pl.when(c == pl.num_programs(0) - 1)
    def _():
        send_packed(pack_ref, g_ref)


def stage_two(f_ref, first_ref, vel_ref, visc_ref, snd_ref, coup_ref, hw_ref, he_ref, gb_ref, ga_ref,
              resp_ref, gram_ref, below_ref, above_ref):
    c = pl.program_id(0)
    ncol = resp_ref.shape[1]
    nx, ny = f_ref.shape[2], f_ref.shape[3]
    receive(c, gb_ref, ga_ref, below_ref, above_ref, ny)
    q = [f_ref[v, 0] + STEP * first_ref[v, 0] for v in range(NV)]
    west = [hw_ref[0, v:v + 1, :] for v in range(NV)]
    east = [he_ref[0, v:v + 1, :] for v in range(NV)]
    lq = operator(q, west, east, below_ref, above_ref, c, vel_ref, visc_ref, snd_ref, coup_ref)
    resp = []
    for v in range(NV):
        forcing = f_ref[v, 0]
        second = lq[v] + forcing
        r = forcing + 0.5 * STEP * (first_ref[v, 0] + second)
        resp_ref[v, pl.ds(c, 1)] = r[None]
        resp.append(r)
    for d in range(ncol):
        @pl.when(d <= c)
        def _():
            acc = None
            for v in range(NV):
                prod = (resp_ref[v, d] * resp[v]).reshape(nx // 8, 8, ny).sum(axis=0)
                acc = prod if acc is None else acc + prod
            row = jnp.sum(acc, axis=0, keepdims=True)
            gram_ref[pl.ds(c * ncol + d, 1), :] = row
            gram_ref[pl.ds(d * ncol + c, 1), :] = row


def edges(f_ref, w_ref, e_ref, g_ref, pack_ref):
    ncol, nx = f_ref.shape[1], f_ref.shape[2]
    for c in range(ncol):
        fields = [f_ref[v, c] for v in range(NV)]
        for v in range(NV):
            w_ref[c, v:v + 1, :] = fields[v][0:1, :]
            e_ref[c, v:v + 1, :] = fields[v][nx - 1:nx, :]
        pack(pack_ref, fields, c)
    send_packed(pack_ref, g_ref)


def combine(inv_ref, r_ref, out_ref):
    ncol = r_ref.shape[1]
    rs = [r_ref[0, d] for d in range(ncol)]
    for c in range(ncol):
        acc = inv_ref[c, 0] * rs[0]
        for d in range(1, ncol):
            acc = acc + inv_ref[c, d] * rs[d]
        out_ref[0, c] = acc


def local(forcing, velocity, viscosity, sound, coupling):
    nv, ncol, nx, ny = forcing.shape
    f32 = jnp.float32
    whole = lambda shape: pl.BlockSpec(shape, lambda c: (0,) * len(shape))
    column = pl.BlockSpec((nv, 1, nx, ny), lambda c: (0, c, 0, 0))
    edge_x = pl.BlockSpec((1, nv, ny), lambda c: (c, 0, 0))
    coef_specs = [whole((2, nx, ny)), whole((nx, ny)), whole((nx, ny)), whole((nv, nv, nx, ny))]
    params = pltpu.CompilerParams(vmem_limit_bytes=60 * 1024 * 1024)

    width = 2 * nv * ncol
    packed = whole((width, nx))
    packed_shape = jax.ShapeDtypeStruct((width, nx), f32)
    tile = pltpu.VMEM((nx, ny), f32)
    fw, fe, fg = pl.pallas_call(
        edges,
        in_specs=[pl.BlockSpec(memory_space=pltpu.VMEM)],
        out_specs=[pl.BlockSpec(memory_space=pltpu.VMEM)] * 3,
        out_shape=[
            jax.ShapeDtypeStruct((ncol, nv, ny), f32),
            jax.ShapeDtypeStruct((ncol, nv, ny), f32),
            packed_shape,
        ],
        scratch_shapes=[tile],
        compiler_params=params,
    )(forcing)
    hw, he = exchange(fw, fe, "gx")
    gb, ga = exchange(fg, fg, "gy")

    first, mw, me, mg = pl.pallas_call(
        stage_one,
        grid=(ncol,),
        in_specs=[column] + coef_specs + [edge_x, edge_x, packed, packed],
        out_specs=[column, edge_x, edge_x, packed],
        out_shape=[
            jax.ShapeDtypeStruct(forcing.shape, f32),
            jax.ShapeDtypeStruct((ncol, nv, ny), f32),
            jax.ShapeDtypeStruct((ncol, nv, ny), f32),
            packed_shape,
        ],
        scratch_shapes=[tile, tile, tile],
        compiler_params=params,
    )(forcing, velocity, viscosity, sound, coupling, hw, he, gb, ga)

    hw2, he2 = exchange(mw, me, "gx")
    gb2, ga2 = exchange(mg, mg, "gy")

    response, partial = pl.pallas_call(
        stage_two,
        grid=(ncol,),
        in_specs=[column, column] + coef_specs + [edge_x, edge_x, packed, packed],
        out_specs=[whole(forcing.shape), whole((ncol * ncol, ny))],
        out_shape=[
            jax.ShapeDtypeStruct(forcing.shape, f32),
            jax.ShapeDtypeStruct((ncol * ncol, ny), f32),
        ],
        compiler_params=pltpu.CompilerParams(
            vmem_limit_bytes=60 * 1024 * 1024, dimension_semantics=("arbitrary",)
        ),
        scratch_shapes=[tile, tile],
    )(forcing, first, velocity, viscosity, sound, coupling, hw2, he2, gb2, ga2)

    rows_total = float(nv * nx * ny * lax.axis_size("gx") * lax.axis_size("gy"))
    local_gram = jnp.sum(partial, axis=1).reshape(ncol, ncol) / rows_total
    lower = jnp.linalg.cholesky(all_sum(local_gram))
    identity = jnp.eye(lower.shape[0], dtype=lower.dtype)
    inverse = lax.linalg.triangular_solve(lower, identity, left_side=True, lower=True)

    basis = pl.pallas_call(
        combine,
        grid=(nv,),
        in_specs=[
            pl.BlockSpec(memory_space=pltpu.SMEM),
            pl.BlockSpec((1, ncol, nx, ny), lambda v: (v, 0, 0, 0)),
        ],
        out_specs=pl.BlockSpec((1, ncol, nx, ny), lambda v: (v, 0, 0, 0)),
        out_shape=jax.ShapeDtypeStruct(forcing.shape, f32),
        compiler_params=params,
    )(inverse, response)
    return (basis, lower.T)


def solution(mesh):
    in_specs = (
        P(None, None, "gx", "gy"),
        P(None, "gx", "gy"),
        P("gx", "gy"),
        P("gx", "gy"),
        P(None, None, "gx", "gy"),
    )
    out_specs = (P(None, None, "gx", "gy"), P())
    return jax.shard_map(local, mesh=mesh, in_specs=in_specs, out_specs=out_specs, check_vma=False)
```
